256 devices in a mesh: seq: 32 (over y, x, core), dev: 8 (over z).
Axes of the slice: x: 4, y: 4, z: 8, core: 2. Of those that a mesh axis runs over, the one named last changes fastest.
Arguments:
- queries: bfloat16 [2048, 4096], P('seq', 'dev'), may hold values from -6 to 6
- key_vectors: bfloat16 [2048, 4096], P('seq', 'dev'), may hold values from -6 to 6
- value_vectors: bfloat16 [2048, 4096], P('seq', 'dev'), may hold values from -6 to 6
- log_decay: float32 [2048, 32], P('seq', 'dev')
- head_gain: float32 [4096], P('dev'), may hold values from 0.5 to 1.5
- gate_weight: bfloat16 [8, 4096, 4096], P('dev', None, 'seq'), may hold values from -0.09375 to 0.09375
- up_weight: bfloat16 [8, 4096, 4096], P('dev', None, 'seq'), may hold values from -0.09375 to 0.09375
- down_weight: bfloat16 [8, 4096, 4096], P('dev', 'seq'), may hold values from -0.0625 to 0.0625
- expert_ids: int32 [2048, 2], P(('seq', 'dev')), may hold values from 0 to 3, all different within a row; in each aligned block of 8 rows (0 to 7, 8 to 15, ...) at most 6 rows name the same one
- expert_weights: float32 [2048, 2], P(('seq', 'dev')), may hold values from 0.2 to 1
Outputs:
- layer_output: bfloat16 [2048, 4096], P(('seq', 'dev'))
The draws below stay inside these ranges and needn't reach their ends.
Inputs may be any that keep to these rules, and one draw needn't show every extreme that they name: `expert_ids`: in each aligned block of 8 rows (the tokens of one device) no expert is named by more than 6 rows, a bound that some block reaches; the two experts of a row differ.
All inputs are finite; a program needn't handle non-finite values.
Results may differ from the reference program's by a relative error of at most 0.03.
Values may be sent and summed in bfloat16 or wider, within the bound.
No kernel may reach another device: no remote copies, remote signals or barrier semaphores. Data moves between devices by JAX's collectives and lax.ppermute only.
A program may use at most 128 MiB of HBM per device.

```python
import math
import jax
import jax.numpy as jnp
import numpy as np
from jax import lax

TOK_DEV = 8
DH = 128
PAIR = 2
TOP = 2
FF_DEV = 128
HEAD_TOTAL = 32
D = 4096
EXPERTS = 4
FF_PAIR = 4096
FF = 8192
SEQ_LEN = 64
BLOCK = 64
TOKEN_TOTAL = 2048
CAP = 6
N_SEQ = 32


def draw_log_decay(key, part):
    random_subkeys = jax.random.split(jax.random.fold_in(key, 17), 7)
    group_count = TOKEN_TOTAL // SEQ_LEN
    fast_share = 0.5
    fast_head = jax.random.uniform(random_subkeys[0], (HEAD_TOTAL,)) < fast_share
    fast_rate = jax.random.uniform(random_subkeys[1], (HEAD_TOTAL,), minval=1.0 / 50.0, maxval=1.0 / 30.0)
    slow_rate = jax.random.uniform(random_subkeys[2], (HEAD_TOTAL,), minval=0.2, maxval=0.6) / TOKEN_TOTAL
    base_rate = jnp.where(fast_head, fast_rate, slow_rate)
    group_factor = jax.random.uniform(random_subkeys[3], (group_count, HEAD_TOTAL), minval=0.6, maxval=1.3)
    roughness = jax.random.uniform(random_subkeys[4], (TOKEN_TOTAL, HEAD_TOTAL), minval=0.5, maxval=1.5)
    group_of_row = jnp.arange(TOKEN_TOTAL) // SEQ_LEN
    decay_speed = base_rate[None, :] * group_factor[group_of_row] * roughness
    spike_location = jax.random.randint(random_subkeys[5], (2, HEAD_TOTAL), 0, TOKEN_TOTAL)
    spike_depth = jax.random.uniform(random_subkeys[6], (2, HEAD_TOTAL), minval=0.2, maxval=0.5)
    row_number = jnp.arange(TOKEN_TOTAL)[:, None]
    spike_summand = jnp.where(row_number == spike_location[0][None, :], jnp.log(1.0 - spike_depth[0])[None, :], 0.0)
    spike_summand = spike_summand + jnp.where(row_number == spike_location[1][None, :], jnp.log(1.0 - spike_depth[1])[None, :], 0.0)
    return (spike_summand - decay_speed).astype(jnp.float32)


def block_levels(key, extent, cuts, smallest, largest):
    level = 1.0
    for axis_at, shards_of in cuts:
        heights = jax.random.uniform(jax.random.fold_in(jax.random.fold_in(key, 6), axis_at), (shards_of,), jnp.float32, smallest / len(cuts), largest / len(cuts))
        level = level * jnp.repeat(jnp.exp(heights), extent[axis_at] // shards_of).reshape((-1,) + (1,) * (len(extent) - 1 - axis_at))
    return level


def routed_block(stream_key, own, number, rows, count, top, reach, lean):
    sequence = jax.random.permutation(stream_key, count)
    heavy_load, ordinary = load_shares(count, rows * top, reach, lean, True), load_shares(count, rows * top, reach, lean, False)
    places = jnp.arange(count)

    def named(sizes, offset_by):
        used = int((sizes > 0).sum())
        fixed = max(1, used // 4)
        moved = fixed + (places - fixed + offset_by * (used - fixed)) % max(1, count - fixed)
        return jnp.zeros((count,), jnp.int32).at[sequence[jnp.where(places < fixed, places, moved)]].set(jnp.asarray(sizes, jnp.int32))

    sizes = jnp.where(number % 4 == 0, named(heavy_load, number // 4), named(ordinary, number - number // 4 - 1))
    mixed = jax.random.permutation(jax.random.fold_in(own, 3), count)
    source_of, receiver = mixed[0:count // 2 * 2:2], mixed[1:count // 2 * 2:2]
    margin = jnp.minimum(sizes[source_of] - 1, reach - sizes[receiver]) // 2
    margin = jnp.where((source_of == sequence[0]) | (receiver == sequence[0]) | (sizes[receiver] == 0), 0, jnp.maximum(margin, 0))
    moved = jax.random.randint(jax.random.fold_in(own, 4), (count // 2,), 0, 1 << 20) % (margin + 1)
    sizes = sizes.at[source_of].add(-moved).at[receiver].add(moved)
    items = jnp.searchsorted(jnp.cumsum(sizes), jnp.arange(rows * top), side="right").astype(jnp.int32)
    grid = items.reshape(top, rows).T
    grid = grid[jax.random.permutation(jax.random.fold_in(own, 1), rows)]
    offset_by = jax.random.randint(jax.random.fold_in(own, 2), (rows, 1), 0, top)
    return jnp.take_along_axis(grid, (jnp.arange(top)[None, :] + offset_by) % top, axis=1)


def load_shares(count, total, bound, skew, full):
    portions = [(1 << 20) // math.isqrt(grade ** skew) + 1 for grade in range(1, count + 1)]
    largest = bound if full else min(bound, max(-(-total // count), total * portions[0] // sum(portions)))
    least = 1 if total - largest >= count - 1 else 0
    holding, rest = [largest] + [least] * (count - 1), total - largest - least * (count - 1)
    while rest > 0:
        free = [i for i in range(1, count) if holding[i] < largest] or [i for i in range(1, count) if holding[i] < bound]
        pool, left = sum([portions[i] for i in free]), rest
        for i in free:
            more = min(bound - holding[i], max(1, left * portions[i] // pool), rest)
            holding[i] = holding[i] + more
            rest = rest - more
    return np.array(holding)


def normal_values(own_key, extent, scale, reach, cuts=(), kind=jnp.bfloat16):
    drawn = jax.random.normal(own_key, extent, jnp.float32) * scale
    if len(cuts) > 0:
        drawn = block_levels(own_key, extent, cuts, -0.22, 0.18) * drawn
    return jnp.clip(drawn, min=-reach, max=reach).astype(kind)


def setup_inputs(seed: int = 0) -> dict:
    key_of = jax.random.split(jax.random.key(seed), 11)
    queries = normal_values(key_of[0], (TOKEN_TOTAL, D), 1.0, 6.0, ((0, 32), (1, 8)))
    key_vectors = normal_values(key_of[1], (TOKEN_TOTAL, D), 1.0, 6.0, ((0, 32), (1, 8)))
    value_vectors = normal_values(key_of[2], (TOKEN_TOTAL, D), 1.0, 6.0, ((0, 32), (1, 8)))
    log_decay = draw_log_decay(jax.random.fold_in(key_of[10], 71), 0)
    head_gain = jnp.clip(1.0 + 0.1 * jax.random.normal(key_of[4], (D,), jnp.float32), 0.5, 1.5)
    gate_weight = normal_values(key_of[5], (EXPERTS * PAIR, D, FF_PAIR), D ** -0.5, 0.09375, ((0, 8), (2, 32)))
    up_weight = normal_values(key_of[6], (EXPERTS * PAIR, D, FF_PAIR), D ** -0.5, 0.09375, ((0, 8), (2, 32)))
    down_weight = normal_values(key_of[7], (EXPERTS * PAIR, FF_PAIR, D), FF ** -0.5, 0.0625, ((0, 8), (1, 32)))
    expert_ids_keys = jax.random.split(jax.random.fold_in(key_of[8], 1), TOKEN_TOTAL // TOK_DEV)
    expert_ids_turns = jax.random.permutation(jax.random.fold_in(key_of[8], 3), TOKEN_TOTAL // TOK_DEV)
    expert_ids = jax.vmap(lambda own, number: routed_block(jax.random.fold_in(key_of[8], 2), own, number, TOK_DEV, EXPERTS, TOP, CAP, 2))(expert_ids_keys, expert_ids_turns).reshape((TOKEN_TOTAL, TOP))
    expert_weights = jnp.clip(0.2 + 0.8 * jax.random.uniform(key_of[9], (TOKEN_TOTAL, TOP), jnp.float32) ** block_levels(key_of[9], (TOKEN_TOTAL, TOP), ((0, 256),), -0.2, 0.2), 0.2, 1.0)
    return {"queries": queries, "key_vectors": key_vectors, "value_vectors": value_vectors, "log_decay": log_decay, "head_gain": head_gain, "gate_weight": gate_weight, "up_weight": up_weight, "down_weight": down_weight, "expert_ids": expert_ids, "expert_weights": expert_weights}


highest = lax.Precision.HIGHEST

def block_step(state, pieces):
    queries_blk, keys_blk, values_blk, decay_blk = pieces
    length = decay_blk.shape[0]
    running = jnp.cumsum(decay_blk)
    causal = jnp.arange(length)[:, None] >= jnp.arange(length)[None, :]
    spread = jnp.where(causal, running[:, None] - running[None, :], 0.0)
    factors = jnp.where(causal, jnp.exp(spread), 0.0)
    scores = jnp.dot(queries_blk, keys_blk.T, preferred_element_type=jnp.float32) * factors
    values_f = values_blk.astype(jnp.float32)
    keys_f = keys_blk.astype(jnp.float32)
    carried = jnp.exp(running)[:, None] * jnp.dot(queries_blk.astype(jnp.float32), state, precision=highest)
    output = jnp.dot(scores, values_f, precision=highest) + carried
    tail_decay = jnp.exp(running[-1] - running)
    state = jnp.exp(running[-1]) * state + jnp.dot((keys_f * tail_decay[:, None]).T, values_f, precision=highest)
    return (state, output)

def run_blocks(state, queries_b, keys_b, values_b, decay_f, block):
    count = decay_f.shape[0] // block
    shaped = (queries_b.reshape(count, block, -1), keys_b.reshape(count, block, -1), values_b.reshape(count, block, -1), decay_f.reshape(count, block))
    state, outputs = lax.scan(block_step, state, shaped)
    return outputs.reshape(count * block, -1)

def head_norm(attention, gain):
    square_mean = lax.optimization_barrier(jnp.mean(attention * attention, axis=-1, keepdims=True))
    return (attention * lax.rsqrt(square_mean + 1e-06) * gain).astype(jnp.bfloat16)

def slot_ranks(flat_experts, experts):
    onehot = (flat_experts[..., None] == jnp.arange(experts, dtype=jnp.int32)).astype(jnp.int32)
    before = jnp.cumsum(onehot, axis=-2) - onehot
    return lax.optimization_barrier(jnp.sum(before * onehot, axis=-1))

def reference(queries, key_vectors, value_vectors, log_decay, head_gain, gate_weight, up_weight, down_weight, expert_ids, expert_weights):

    def one_head(head):
        start = head * DH
        head_queries = lax.dynamic_slice_in_dim(queries, start, DH, 1)
        head_keys = lax.dynamic_slice_in_dim(key_vectors, start, DH, 1)
        head_values = lax.dynamic_slice_in_dim(value_vectors, start, DH, 1)
        head_decay = lax.dynamic_slice_in_dim(log_decay, head, 1, 1)[:, 0]
        gain_part = lax.dynamic_slice_in_dim(head_gain, start, DH, 0)
        attention = run_blocks(jnp.zeros((DH, DH), jnp.float32), head_queries, head_keys, head_values, head_decay, BLOCK)
        return head_norm(attention, gain_part)
    per_head = lax.map(one_head, jnp.arange(HEAD_TOTAL, dtype=jnp.int32))
    normed = jnp.transpose(per_head, (1, 0, 2)).reshape(TOKEN_TOTAL, D)
    block_count = TOKEN_TOTAL // TOK_DEV
    per_expert = block_count * CAP
    flat_experts = expert_ids.reshape(block_count, TOK_DEV * TOP)
    slot_rank = slot_ranks(flat_experts, EXPERTS)
    block_index = jnp.arange(block_count, dtype=jnp.int32)[:, None]
    slot_index = flat_experts * per_expert + block_index * CAP + slot_rank
    token_index = block_index * TOK_DEV + jnp.arange(TOK_DEV * TOP, dtype=jnp.int32)[None, :] // TOP
    slot_token = jnp.full((EXPERTS * per_expert,), TOKEN_TOTAL, jnp.int32).at[slot_index.reshape(-1)].set(token_index.reshape(-1))
    slot_weight = jnp.zeros((EXPERTS * per_expert,), jnp.float32).at[slot_index.reshape(-1)].set(expert_weights.reshape(-1))
    padded = jnp.concatenate([normed, jnp.zeros((1, D), normed.dtype)], axis=0)
    piece_count = PAIR * N_SEQ

    def add_expert(total, expert):
        tokens_here = lax.dynamic_slice_in_dim(slot_token, expert * per_expert, per_expert)
        weights_here = lax.dynamic_slice_in_dim(slot_weight, expert * per_expert, per_expert)
        first_row = (expert * PAIR).astype(jnp.int32)
        gate_full = jnp.transpose(lax.dynamic_slice_in_dim(gate_weight, first_row, PAIR, 0), (1, 0, 2)).reshape(D, FF)
        up_full = jnp.transpose(lax.dynamic_slice_in_dim(up_weight, first_row, PAIR, 0), (1, 0, 2)).reshape(D, FF)
        down_pieces = lax.dynamic_slice_in_dim(down_weight, first_row, PAIR, 0).reshape(piece_count, FF_DEV, D)
        picked = padded[tokens_here]
        gate_part = jnp.dot(picked, gate_full, preferred_element_type=jnp.float32)
        up_part = jnp.dot(picked, up_full, preferred_element_type=jnp.float32)
        hidden = (jax.nn.silu(gate_part) * up_part).astype(jnp.bfloat16)

        def add_piece(acc, index):
            hidden_piece = lax.dynamic_slice_in_dim(hidden, index * FF_DEV, FF_DEV, 1)
            term = jnp.dot(hidden_piece, down_pieces[index], preferred_element_type=jnp.float32).astype(jnp.bfloat16)
            term = lax.optimization_barrier(term)
            return (acc + term.astype(jnp.float32), None)
        summed, _ = lax.scan(add_piece, jnp.zeros((per_expert, D), jnp.float32), jnp.arange(piece_count, dtype=jnp.int32))
        result = summed.astype(jnp.bfloat16)
        total = total.at[tokens_here].add(result.astype(jnp.float32) * weights_here[:, None], mode='drop')
        return (total, None)
    total, _ = lax.scan(add_expert, jnp.zeros((TOKEN_TOTAL, D), jnp.float32), jnp.arange(EXPERTS, dtype=jnp.int32))
    return total.astype(jnp.bfloat16)
```

```python
import jax
import jax.numpy as jnp
import numpy as np
from jax import lax
from jax.sharding import Mesh
from jax.sharding import PartitionSpec as P

PAIR = 2

highest = lax.Precision.HIGHEST

SEQ_AXES = ("y", "x", "c")
TOK_AXES = ("y", "x")


def chain_join(earlier, later):
    return (earlier[0] + later[0], jnp.exp(later[0])[:, None, None] * earlier[1] + later[1])


def shifted(value, shift, count):
    pairs = [(i, i + shift) for i in range(count - shift)]
    return lax.ppermute(value, SEQ_AXES, pairs)


def carried_in(log_total, local_state, count):
    state = shifted((log_total, local_state), 1, count)
    shift = 1
    while shift < count - 1:
        state = chain_join(shifted(state, shift, count), state)
        shift *= 2
    return state[1]


def head_norm(attention, gain):
    square_mean = jnp.mean(attention * attention, axis=-1, keepdims=True)
    return (attention * lax.rsqrt(square_mean + 1e-06) * gain).astype(jnp.bfloat16)


def slot_ranks(flat_experts, experts):
    onehot = (flat_experts[..., None] == jnp.arange(experts, dtype=jnp.int32)).astype(jnp.int32)
    before = jnp.cumsum(onehot, axis=-2) - onehot
    return jnp.sum(before * onehot, axis=-1)


def per_device(
    queries,
    key_vectors,
    value_vectors,
    log_decay,
    head_gain,
    gate_weight,
    up_weight,
    down_weight,
    expert_ids,
    expert_weights,
):
    count = 1
    for name in SEQ_AXES:
        count *= lax.axis_size(name)
    dev_count = lax.axis_size("dev")
    experts = dev_count // PAIR

    gate_both = lax.all_gather(gate_weight[0], "c", axis=1, tiled=True)
    up_both = lax.all_gather(up_weight[0], "c", axis=1, tiled=True)
    down_both = lax.all_gather(down_weight[0], "c", axis=0, tiled=True)

    tok_count = expert_ids.shape[0]
    top_count = expert_ids.shape[1]
    capacity = max(2, (3 * tok_count * top_count + 2 * experts - 1) // (2 * experts))
    ids_all = lax.all_gather(expert_ids, "dev", axis=0, tiled=False)

    seq_len = queries.shape[0]
    heads = log_decay.shape[1]
    head_dim = queries.shape[1] // heads
    queries_h = jnp.transpose(queries.reshape(seq_len, heads, head_dim), (1, 0, 2))
    keys_h = jnp.transpose(key_vectors.reshape(seq_len, heads, head_dim), (1, 0, 2))
    values_h = jnp.transpose(value_vectors.reshape(seq_len, heads, head_dim), (1, 0, 2))
    decay_h = jnp.transpose(log_decay, (1, 0))
    running = jnp.cumsum(decay_h, axis=1)
    log_total = running[:, -1]
    tail_decay = jnp.exp(log_total[:, None] - running)
    keys_f = keys_h.astype(jnp.float32)
    values_f = values_h.astype(jnp.float32)
    local_state = jnp.einsum(
        "hsa,hsb->hab", keys_f * tail_decay[:, :, None], values_f, precision=highest
    )
    incoming = carried_in(log_total, local_state, count)

    causal = jnp.arange(seq_len)[:, None] >= jnp.arange(seq_len)[None, :]
    spread = jnp.where(causal[None], running[:, :, None] - running[:, None, :], 0.0)
    factors = jnp.where(causal[None], jnp.exp(spread), 0.0)
    scores = (
        jnp.einsum("hta,hsa->hts", queries_h, keys_h, preferred_element_type=jnp.float32) * factors
    )
    carried = jnp.exp(running)[:, :, None] * jnp.einsum(
        "hta,hab->htb", queries_h.astype(jnp.float32), incoming, precision=highest
    )
    attention = jnp.einsum("hts,hsb->htb", scores, values_f, precision=highest) + carried
    normed_h = head_norm(attention, head_gain.reshape(heads, 1, head_dim))
    normed = jnp.transpose(normed_h, (1, 0, 2)).reshape(seq_len, heads * head_dim)

    per_expert = dev_count * capacity
    flat = ids_all.reshape(dev_count, tok_count * top_count)
    rank = slot_ranks(flat, experts)
    source = jnp.arange(dev_count, dtype=jnp.int32)[:, None]
    slot_index = flat * per_expert + source * capacity + rank
    token_local = source * tok_count + jnp.arange(tok_count * top_count, dtype=jnp.int32)[None, :] // top_count
    slot_token = (
        jnp.full((experts * per_expert,), seq_len, jnp.int32)
        .at[slot_index.reshape(-1)]
        .set(token_local.reshape(-1))
    )
    padded = jnp.concatenate([normed, jnp.zeros((1, normed.shape[1]), normed.dtype)], axis=0)
    send_rows = jnp.repeat(padded[slot_token].reshape(experts, per_expert, -1), PAIR, axis=0)
    arrived = lax.all_to_all(send_rows, "dev", split_axis=0, concat_axis=0, tiled=True)
    local_rows = jnp.transpose(arrived.reshape(dev_count, per_expert, -1), (1, 0, 2)).reshape(
        per_expert, -1
    )
    width = local_rows.shape[1]

    piece = lax.all_gather(local_rows, TOK_AXES, axis=0, tiled=True)
    gate_part = jnp.dot(piece, gate_both, preferred_element_type=jnp.float32)
    up_part = jnp.dot(piece, up_both, preferred_element_type=jnp.float32)
    hidden_all = (jax.nn.silu(gate_part) * up_part).astype(jnp.bfloat16)
    term = jnp.dot(hidden_all, down_both, preferred_element_type=jnp.float32).astype(jnp.bfloat16)
    summed = lax.psum_scatter(term, TOK_AXES, scatter_dimension=0, tiled=True)
    returned = lax.all_to_all(
        summed.reshape(dev_count, capacity, width),
        "dev",
        split_axis=0,
        concat_axis=0,
        tiled=True,
    ).astype(jnp.float32)
    expert_out = jnp.sum(returned.reshape(experts, PAIR, capacity, width), axis=1).astype(
        jnp.bfloat16
    )
    own = lax.axis_index("dev")
    own_flat = lax.dynamic_index_in_dim(flat, own, 0, False)
    own_rank = lax.dynamic_index_in_dim(rank, own, 0, False)
    pick_index = own_flat * capacity + own_rank
    picked = expert_out.reshape(experts * capacity, width)[pick_index].reshape(
        tok_count, top_count, width
    )
    combined = jnp.sum(picked.astype(jnp.float32) * expert_weights[:, :, None], axis=1)
    return combined.astype(jnp.bfloat16)


def split_mesh(mesh):
    devices = mesh.devices
    seq_count, dev_count = devices.shape
    cores = 2
    xs = 4
    flat = devices.reshape(-1)
    if hasattr(flat[0], "coords"):
        cores = len({int(getattr(d, "core_on_chip", 0)) for d in flat})
        xs = len({int(d.coords[0]) for d in flat})
    ys = seq_count // (xs * cores)
    return Mesh(devices.reshape(ys, xs, cores, dev_count), ("y", "x", "c", "dev"))


def solution(mesh):
    fine = split_mesh(mesh)
    seq = SEQ_AXES
    in_specs = (
        P(seq, "dev"),
        P(seq, "dev"),
        P(seq, "dev"),
        P(seq, "dev"),
        P("dev"),
        P("dev", None, seq),
        P("dev", None, seq),
        P("dev", seq, None),
        P(seq + ("dev",), None),
        P(seq + ("dev",), None),
    )
    out_specs = P(seq + ("dev",), None)
    return jax.shard_map(
        per_device, mesh=fine, in_specs=in_specs, out_specs=out_specs, check_vma=False
    )
```

```python
import jax
import jax.numpy as jnp
import numpy as np
from jax import lax
from jax.sharding import Mesh
from jax.sharding import PartitionSpec as P

PAIR = 2

highest = lax.Precision.HIGHEST

SEQ_AXES = ("y", "x", "c")
TOK_AXES = ("y", "x")
DEV_AXES = ("e", "p")
BLOCK_AXES = ("c", "p")


def chain_join(earlier, later):
    scale = jnp.exp(later[:, -1:, :])
    state = scale * earlier[:, :-1, :] + later[:, :-1, :]
    return jnp.concatenate([state, earlier[:, -1:, :] + later[:, -1:, :]], axis=1)


def shifted(value, shift, count):
    pairs = [(i, i + shift) for i in range(count - shift)]
    return lax.ppermute(value, SEQ_AXES, pairs)


def carried_in(log_total, local_state, count):
    width = local_state.shape[-1]
    packed = jnp.concatenate(
        [local_state, jnp.broadcast_to(log_total[:, None, None], (log_total.shape[0], 1, width))],
        axis=1,
    )
    state = shifted(packed, 1, count)
    shift = 1
    while shift < count - 1:
        state = chain_join(shifted(state, shift, count), state)
        shift *= 2
    return state[:, :-1, :]


def head_norm(attention, gain):
    square_mean = jnp.mean(attention * attention, axis=-1, keepdims=True)
    return (attention * lax.rsqrt(square_mean + 1e-06) * gain).astype(jnp.bfloat16)


def slot_ranks(flat_experts, experts):
    onehot = (flat_experts[..., None] == jnp.arange(experts, dtype=jnp.int32)).astype(jnp.int32)
    before = jnp.cumsum(onehot, axis=-2) - onehot
    return jnp.sum(before * onehot, axis=-1)


def per_device(
    queries,
    key_vectors,
    value_vectors,
    log_decay,
    head_gain,
    gate_weight,
    up_weight,
    down_weight,
    expert_ids,
    expert_weights,
):
    count = 1
    for name in SEQ_AXES:
        count *= lax.axis_size(name)
    dev_count = lax.axis_size("e") * lax.axis_size("p")
    experts = dev_count // PAIR

    gate_up = jnp.stack([gate_weight[0], up_weight[0]])
    gate_up = lax.all_gather(gate_up, BLOCK_AXES, axis=2, tiled=True)
    down_all = lax.all_gather(down_weight[0], BLOCK_AXES, axis=0, tiled=True)

    tok_count = expert_ids.shape[0]
    top_count = expert_ids.shape[1]
    capacity = max(2, (3 * tok_count * top_count + 2 * experts - 1) // (2 * experts))
    capacity = -(-capacity // PAIR) * PAIR
    half = capacity // PAIR
    ids_all = lax.all_gather(expert_ids, DEV_AXES, axis=0, tiled=False)

    seq_len = queries.shape[0]
    heads = log_decay.shape[1]
    head_dim = queries.shape[1] // heads
    queries_h = jnp.transpose(queries.reshape(seq_len, heads, head_dim), (1, 0, 2))
    keys_h = jnp.transpose(key_vectors.reshape(seq_len, heads, head_dim), (1, 0, 2))
    values_h = jnp.transpose(value_vectors.reshape(seq_len, heads, head_dim), (1, 0, 2))
    decay_h = jnp.transpose(log_decay, (1, 0))
    running = jnp.cumsum(decay_h, axis=1)
    log_total = running[:, -1]
    tail_decay = jnp.exp(log_total[:, None] - running)
    keys_f = keys_h.astype(jnp.float32)
    values_f = values_h.astype(jnp.float32)
    local_state = jnp.einsum(
        "hsa,hsb->hab", keys_f * tail_decay[:, :, None], values_f, precision=highest
    )
    incoming = carried_in(log_total, local_state, count)

    causal = jnp.arange(seq_len)[:, None] >= jnp.arange(seq_len)[None, :]
    spread = jnp.where(causal[None], running[:, :, None] - running[:, None, :], 0.0)
    factors = jnp.where(causal[None], jnp.exp(spread), 0.0)
    scores = (
        jnp.einsum("hta,hsa->hts", queries_h, keys_h, preferred_element_type=jnp.float32) * factors
    )
    carried = jnp.exp(running)[:, :, None] * jnp.einsum(
        "hta,hab->htb", queries_h.astype(jnp.float32), incoming, precision=highest
    )
    attention = jnp.einsum("hts,hsb->htb", scores, values_f, precision=highest) + carried
    normed_h = head_norm(attention, head_gain.reshape(heads, 1, head_dim))
    normed = jnp.transpose(normed_h, (1, 0, 2)).reshape(seq_len, heads * head_dim)

    per_dev = dev_count * half
    flat = ids_all.reshape(dev_count, tok_count * top_count)
    rank = slot_ranks(flat, experts)
    source = jnp.arange(dev_count, dtype=jnp.int32)[:, None]
    slot_index = (flat * PAIR + rank // half) * per_dev + source * half + rank % half
    token_local = source * tok_count + jnp.arange(tok_count * top_count, dtype=jnp.int32)[None, :] // top_count
    slot_token = (
        jnp.full((dev_count * per_dev,), seq_len, jnp.int32)
        .at[slot_index.reshape(-1)]
        .set(token_local.reshape(-1))
    )
    padded = jnp.concatenate([normed, jnp.zeros((1, normed.shape[1]), normed.dtype)], axis=0)
    send_rows = padded[slot_token].reshape(dev_count, per_dev, -1)
    arrived = lax.all_to_all(send_rows, DEV_AXES, split_axis=0, concat_axis=0, tiled=True)
    local_rows = jnp.transpose(arrived, (1, 0, 2)).reshape(per_dev, -1)
    width = local_rows.shape[1]
    gate_up, down_all, local_rows = lax.optimization_barrier((gate_up, down_all, local_rows))

    piece = lax.all_gather(local_rows, TOK_AXES, axis=0, tiled=True)
    gate_part = jnp.dot(piece, gate_up[0], preferred_element_type=jnp.float32)
    up_part = jnp.dot(piece, gate_up[1], preferred_element_type=jnp.float32)
    hidden_all = (jax.nn.silu(gate_part) * up_part).astype(jnp.bfloat16)
    term = jnp.dot(hidden_all, down_all, preferred_element_type=jnp.float32).astype(jnp.bfloat16)
    summed = lax.psum_scatter(term, TOK_AXES, scatter_dimension=0, tiled=True)
    returned = lax.all_to_all(
        summed.reshape(dev_count, half, width),
        DEV_AXES,
        split_axis=0,
        concat_axis=0,
        tiled=True,
    )
    own = lax.axis_index(DEV_AXES)
    own_flat = lax.dynamic_index_in_dim(flat, own, 0, False)
    own_rank = lax.dynamic_index_in_dim(rank, own, 0, False)
    pick_index = own_flat * capacity + own_rank
    picked = returned.reshape(dev_count * half, width)[pick_index].reshape(
        tok_count, top_count, width
    )
    combined = jnp.sum(picked.astype(jnp.float32) * expert_weights[:, :, None], axis=1)
    return combined.astype(jnp.bfloat16)


def split_mesh(mesh):
    devices = mesh.devices
    seq_count, dev_count = devices.shape
    cores = 2
    xs = 4
    flat = devices.reshape(-1)
    if hasattr(flat[0], "coords"):
        cores = len({int(getattr(d, "core_on_chip", 0)) for d in flat})
        xs = len({int(d.coords[0]) for d in flat})
    ys = seq_count // (xs * cores)
    shape = (ys, xs, cores, dev_count // PAIR, PAIR)
    return Mesh(devices.reshape(shape), ("y", "x", "c", "e", "p"))


def solution(mesh):
    fine = split_mesh(mesh)
    seq = SEQ_AXES
    in_specs = (
        P(seq, DEV_AXES),
        P(seq, DEV_AXES),
        P(seq, DEV_AXES),
        P(seq, DEV_AXES),
        P(DEV_AXES),
        P(DEV_AXES, None, seq),
        P(DEV_AXES, None, seq),
        P(DEV_AXES, seq, None),
        P(seq + DEV_AXES, None),
        P(seq + DEV_AXES, None),
    )
    out_specs = P(seq + DEV_AXES, None)
    return jax.shard_map(
        per_device, mesh=fine, in_specs=in_specs, out_specs=out_specs, check_vma=False
    )
```

```python
import jax
import jax.numpy as jnp
import numpy as np
from jax import lax
from jax.sharding import Mesh
from jax.sharding import PartitionSpec as P

PAIR = 2

highest = lax.Precision.HIGHEST

SEQ_AXES = ("y", "x", "c")
TOK_AXES = ("y", "x")


def chain_join(earlier, later):
    scale = jnp.exp(later[:, -1:, :])
    state = scale * earlier[:, :-1, :] + later[:, :-1, :]
    return jnp.concatenate([state, earlier[:, -1:, :] + later[:, -1:, :]], axis=1)


def shifted(value, shift, count):
    pairs = [(i, i + shift) for i in range(count - shift)]
    return lax.ppermute(value, SEQ_AXES, pairs)


def carried_in(log_total, local_state, count):
    width = local_state.shape[-1]
    packed = jnp.concatenate(
        [local_state, jnp.broadcast_to(log_total[:, None, None], (log_total.shape[0], 1, width))],
        axis=1,
    )
    state = shifted(packed, 1, count)
    shift = 1
    while shift < count - 1:
        state = chain_join(shifted(state, shift, count), state)
        shift *= 2
    return state[:, :-1, :]


def head_norm(attention, gain):
    square_mean = jnp.mean(attention * attention, axis=-1, keepdims=True)
    return (attention * lax.rsqrt(square_mean + 1e-06) * gain).astype(jnp.bfloat16)


def slot_ranks(flat_experts, experts):
    onehot = (flat_experts[..., None] == jnp.arange(experts, dtype=jnp.int32)).astype(jnp.int32)
    before = jnp.cumsum(onehot, axis=-2) - onehot
    return jnp.sum(before * onehot, axis=-1)


def per_device(
    queries,
    key_vectors,
    value_vectors,
    log_decay,
    head_gain,
    gate_weight,
    up_weight,
    down_weight,
    expert_ids,
    expert_weights,
):
    count = 1
    for name in SEQ_AXES:
        count *= lax.axis_size(name)
    dev_count = lax.axis_size("dev")
    experts = dev_count // PAIR

    gate_both = lax.all_gather(gate_weight[0], "c", axis=1, tiled=True)
    up_both = lax.all_gather(up_weight[0], "c", axis=1, tiled=True)
    down_both = lax.all_gather(down_weight[0], "c", axis=0, tiled=True)

    tok_count = expert_ids.shape[0]
    top_count = expert_ids.shape[1]
    capacity = max(2, (3 * tok_count * top_count + 2 * experts - 1) // (2 * experts))
    ids_all = lax.all_gather(expert_ids, "dev", axis=0, tiled=False)

    seq_len = queries.shape[0]
    heads = log_decay.shape[1]
    head_dim = queries.shape[1] // heads
    queries_h = jnp.transpose(queries.reshape(seq_len, heads, head_dim), (1, 0, 2))
    keys_h = jnp.transpose(key_vectors.reshape(seq_len, heads, head_dim), (1, 0, 2))
    values_h = jnp.transpose(value_vectors.reshape(seq_len, heads, head_dim), (1, 0, 2))
    decay_h = jnp.transpose(log_decay, (1, 0))
    running = jnp.cumsum(decay_h, axis=1)
    log_total = running[:, -1]
    tail_decay = jnp.exp(log_total[:, None] - running)
    keys_f = keys_h.astype(jnp.float32)
    values_f = values_h.astype(jnp.float32)
    local_state = jnp.einsum(
        "hsa,hsb->hab", keys_f * tail_decay[:, :, None], values_f, precision=highest
    )
    incoming = carried_in(log_total, local_state, count)

    causal = jnp.arange(seq_len)[:, None] >= jnp.arange(seq_len)[None, :]
    spread = jnp.where(causal[None], running[:, :, None] - running[:, None, :], 0.0)
    factors = jnp.where(causal[None], jnp.exp(spread), 0.0)
    scores = (
        jnp.einsum("hta,hsa->hts", queries_h, keys_h, preferred_element_type=jnp.float32) * factors
    )
    carried = jnp.exp(running)[:, :, None] * jnp.einsum(
        "hta,hab->htb", queries_h.astype(jnp.float32), incoming, precision=highest
    )
    attention = jnp.einsum("hts,hsb->htb", scores, values_f, precision=highest) + carried
    normed_h = head_norm(attention, head_gain.reshape(heads, 1, head_dim))
    normed = jnp.transpose(normed_h, (1, 0, 2)).reshape(seq_len, heads * head_dim)

    per_expert = dev_count * capacity
    flat = ids_all.reshape(dev_count, tok_count * top_count)
    rank = slot_ranks(flat, experts)
    source = jnp.arange(dev_count, dtype=jnp.int32)[:, None]
    slot_index = flat * per_expert + source * capacity + rank
    token_local = source * tok_count + jnp.arange(tok_count * top_count, dtype=jnp.int32)[None, :] // top_count
    slot_token = (
        jnp.full((experts * per_expert,), seq_len, jnp.int32)
        .at[slot_index.reshape(-1)]
        .set(token_local.reshape(-1))
    )
    padded = jnp.concatenate([normed, jnp.zeros((1, normed.shape[1]), normed.dtype)], axis=0)
    send_rows = jnp.repeat(padded[slot_token].reshape(experts, per_expert, -1), PAIR, axis=0)
    arrived = lax.all_to_all(send_rows, "dev", split_axis=0, concat_axis=0, tiled=True)
    local_rows = jnp.transpose(arrived.reshape(dev_count, per_expert, -1), (1, 0, 2)).reshape(
        per_expert, -1
    )
    width = local_rows.shape[1]
    gate_both, up_both, down_both, local_rows = lax.optimization_barrier(
        (gate_both, up_both, down_both, local_rows)
    )
    groups = 1
    for name in TOK_AXES:
        groups *= lax.axis_size(name)
    piece = lax.all_to_all(
        jnp.broadcast_to(local_rows[None], (groups,) + local_rows.shape),
        TOK_AXES,
        split_axis=0,
        concat_axis=0,
        tiled=True,
    ).reshape(groups * per_expert, width)
    gate_part = jnp.dot(piece, gate_both, preferred_element_type=jnp.float32)
    up_part = jnp.dot(piece, up_both, preferred_element_type=jnp.float32)
    hidden_all = (jax.nn.silu(gate_part) * up_part).astype(jnp.bfloat16)
    term = jnp.dot(hidden_all, down_both, preferred_element_type=jnp.float32).astype(jnp.bfloat16)
    parts = lax.all_to_all(
        term.reshape(groups, per_expert, width), TOK_AXES, split_axis=0, concat_axis=0, tiled=True
    )
    summed = jnp.sum(parts.astype(jnp.float32), axis=0).astype(jnp.bfloat16)
    returned = lax.all_to_all(
        summed.reshape(dev_count, capacity, width),
        "dev",
        split_axis=0,
        concat_axis=0,
        tiled=True,
    ).astype(jnp.float32)
    expert_out = jnp.sum(returned.reshape(experts, PAIR, capacity, width), axis=1).astype(
        jnp.bfloat16
    )
    own = lax.axis_index("dev")
    own_flat = lax.dynamic_index_in_dim(flat, own, 0, False)
    own_rank = lax.dynamic_index_in_dim(rank, own, 0, False)
    pick_index = own_flat * capacity + own_rank
    picked = expert_out.reshape(experts * capacity, width)[pick_index].reshape(
        tok_count, top_count, width
    )
    combined = jnp.sum(picked.astype(jnp.float32) * expert_weights[:, :, None], axis=1)
    return combined.astype(jnp.bfloat16)


def split_mesh(mesh):
    devices = mesh.devices
    seq_count, dev_count = devices.shape
    cores = 2
    xs = 4
    flat = devices.reshape(-1)
    if hasattr(flat[0], "coords"):
        cores = len({int(getattr(d, "core_on_chip", 0)) for d in flat})
        xs = len({int(d.coords[0]) for d in flat})
    ys = seq_count // (xs * cores)
    return Mesh(devices.reshape(ys, xs, cores, dev_count), ("y", "x", "c", "dev"))


def solution(mesh):
    fine = split_mesh(mesh)
    seq = SEQ_AXES
    in_specs = (
        P(seq, "dev"),
        P(seq, "dev"),
        P(seq, "dev"),
        P(seq, "dev"),
        P("dev"),
        P("dev", None, seq),
        P("dev", None, seq),
        P("dev", seq, None),
        P(seq + ("dev",), None),
        P(seq + ("dev",), None),
    )
    out_specs = P(seq + ("dev",), None)
    return jax.shard_map(
        per_device, mesh=fine, in_specs=in_specs, out_specs=out_specs, check_vma=False
    )
```

```python
import jax
import jax.numpy as jnp
import numpy as np
from jax import lax
from jax.sharding import Mesh
from jax.sharding import PartitionSpec as P

PAIR = 2

highest = lax.Precision.HIGHEST

SEQ_AXES = ("y", "x", "c")
TOK_AXES = ("y", "x")
DEV_AXES = ("e", "p")


def chain_join(earlier, later):
    scale = jnp.exp(later[:, -1:, :])
    state = scale * earlier[:, :-1, :] + later[:, :-1, :]
    return jnp.concatenate([state, earlier[:, -1:, :] + later[:, -1:, :]], axis=1)


def shifted(value, shift, count):
    pairs = [(i, i + shift) for i in range(count - shift)]
    return lax.ppermute(value, SEQ_AXES, pairs)


def carried_in(log_total, local_state, count):
    width = local_state.shape[-1]
    packed = jnp.concatenate(
        [local_state, jnp.broadcast_to(log_total[:, None, None], (log_total.shape[0], 1, width))],
        axis=1,
    )
    state = shifted(packed, 1, count)
    shift = 1
    while shift < count - 1:
        state = chain_join(shifted(state, shift, count), state)
        shift *= 2
    return state[:, :-1, :]


def head_norm(attention, gain):
    square_mean = jnp.mean(attention * attention, axis=-1, keepdims=True)
    return (attention * lax.rsqrt(square_mean + 1e-06) * gain).astype(jnp.bfloat16)


def slot_ranks(flat_experts, experts):
    onehot = (flat_experts[..., None] == jnp.arange(experts, dtype=jnp.int32)).astype(jnp.int32)
    before = jnp.cumsum(onehot, axis=-2) - onehot
    return jnp.sum(before * onehot, axis=-1)


def per_device(
    queries,
    key_vectors,
    value_vectors,
    log_decay,
    head_gain,
    gate_weight,
    up_weight,
    down_weight,
    expert_ids,
    expert_weights,
):
    count = 1
    for name in SEQ_AXES:
        count *= lax.axis_size(name)
    dev_count = lax.axis_size("e") * lax.axis_size("p")
    experts = dev_count // PAIR

    partner = [(0, 1), (1, 0)]
    gate_up = jnp.stack([gate_weight[0], up_weight[0]])
    gate_up = jnp.concatenate([gate_up, lax.ppermute(gate_up, "p", partner)], axis=2)
    down_all = jnp.concatenate([down_weight[0], lax.ppermute(down_weight[0], "p", partner)], axis=0)

    tok_count = expert_ids.shape[0]
    top_count = expert_ids.shape[1]
    capacity = max(2, (3 * tok_count * top_count + 2 * experts - 1) // (2 * experts))
    capacity = -(-capacity // PAIR) * PAIR
    half = capacity // PAIR
    ids_all = lax.all_gather(expert_ids, DEV_AXES, axis=0, tiled=False)

    seq_len = queries.shape[0]
    heads = log_decay.shape[1]
    head_dim = queries.shape[1] // heads
    queries_h = jnp.transpose(queries.reshape(seq_len, heads, head_dim), (1, 0, 2))
    keys_h = jnp.transpose(key_vectors.reshape(seq_len, heads, head_dim), (1, 0, 2))
    values_h = jnp.transpose(value_vectors.reshape(seq_len, heads, head_dim), (1, 0, 2))
    decay_h = jnp.transpose(log_decay, (1, 0))
    running = jnp.cumsum(decay_h, axis=1)
    log_total = running[:, -1]
    tail_decay = jnp.exp(log_total[:, None] - running)
    keys_f = keys_h.astype(jnp.float32)
    values_f = values_h.astype(jnp.float32)
    local_state = jnp.einsum(
        "hsa,hsb->hab", keys_f * tail_decay[:, :, None], values_f, precision=highest
    )
    incoming = carried_in(log_total, local_state, count)

    causal = jnp.arange(seq_len)[:, None] >= jnp.arange(seq_len)[None, :]
    spread = jnp.where(causal[None], running[:, :, None] - running[:, None, :], 0.0)
    factors = jnp.where(causal[None], jnp.exp(spread), 0.0)
    scores = (
        jnp.einsum("hta,hsa->hts", queries_h, keys_h, preferred_element_type=jnp.float32) * factors
    )
    carried = jnp.exp(running)[:, :, None] * jnp.einsum(
        "hta,hab->htb", queries_h.astype(jnp.float32), incoming, precision=highest
    )
    attention = jnp.einsum("hts,hsb->htb", scores, values_f, precision=highest) + carried
    normed_h = head_norm(attention, head_gain.reshape(heads, 1, head_dim))
    normed = jnp.transpose(normed_h, (1, 0, 2)).reshape(seq_len, heads * head_dim)

    per_dev = dev_count * half
    flat = ids_all.reshape(dev_count, tok_count * top_count)
    rank = slot_ranks(flat, experts)
    source = jnp.arange(dev_count, dtype=jnp.int32)[:, None]
    slot_index = (flat * PAIR + rank // half) * per_dev + source * half + rank % half
    token_local = source * tok_count + jnp.arange(tok_count * top_count, dtype=jnp.int32)[None, :] // top_count
    slot_token = (
        jnp.full((dev_count * per_dev,), seq_len, jnp.int32)
        .at[slot_index.reshape(-1)]
        .set(token_local.reshape(-1))
    )
    padded = jnp.concatenate([normed, jnp.zeros((1, normed.shape[1]), normed.dtype)], axis=0)
    send_rows = padded[slot_token].reshape(dev_count, per_dev, -1)
    gate_up, down_all, send_rows = lax.optimization_barrier((gate_up, down_all, send_rows))
    gate_up = lax.all_gather(gate_up, "c", axis=2, tiled=True)
    down_all = lax.all_gather(down_all, "c", axis=0, tiled=True)
    arrived = lax.all_to_all(send_rows, DEV_AXES, split_axis=0, concat_axis=0, tiled=True)
    local_rows = jnp.transpose(arrived, (1, 0, 2)).reshape(per_dev, -1)
    width = local_rows.shape[1]
    groups = 1
    for name in TOK_AXES:
        groups *= lax.axis_size(name)
    piece = lax.all_to_all(
        jnp.broadcast_to(local_rows[None], (groups,) + local_rows.shape),
        TOK_AXES,
        split_axis=0,
        concat_axis=0,
        tiled=True,
    ).reshape(groups * per_dev, width)
    gate_part = jnp.dot(piece, gate_up[0], preferred_element_type=jnp.float32)
    up_part = jnp.dot(piece, gate_up[1], preferred_element_type=jnp.float32)
    hidden_all = (jax.nn.silu(gate_part) * up_part).astype(jnp.bfloat16)
    term = jnp.dot(hidden_all, down_all, preferred_element_type=jnp.float32).astype(jnp.bfloat16)
    parts = lax.all_to_all(
        term.reshape(groups, per_dev, width), TOK_AXES, split_axis=0, concat_axis=0, tiled=True
    )
    summed = jnp.sum(parts.astype(jnp.float32), axis=0).astype(jnp.bfloat16)
    returned = lax.all_to_all(
        summed.reshape(dev_count, half, width),
        DEV_AXES,
        split_axis=0,
        concat_axis=0,
        tiled=True,
    )
    own = lax.axis_index(DEV_AXES)
    own_flat = lax.dynamic_index_in_dim(flat, own, 0, False)
    own_rank = lax.dynamic_index_in_dim(rank, own, 0, False)
    pick_index = own_flat * capacity + own_rank
    picked = returned.reshape(dev_count * half, width)[pick_index].reshape(
        tok_count, top_count, width
    )
    combined = jnp.sum(picked.astype(jnp.float32) * expert_weights[:, :, None], axis=1)
    return combined.astype(jnp.bfloat16)


def split_mesh(mesh):
    devices = mesh.devices
    seq_count, dev_count = devices.shape
    cores = 2
    xs = 4
    flat = devices.reshape(-1)
    if hasattr(flat[0], "coords"):
        cores = len({int(getattr(d, "core_on_chip", 0)) for d in flat})
        xs = len({int(d.coords[0]) for d in flat})
    ys = seq_count // (xs * cores)
    shape = (ys, xs, cores, dev_count // PAIR, PAIR)
    return Mesh(devices.reshape(shape), ("y", "x", "c", "e", "p"))


def solution(mesh):
    fine = split_mesh(mesh)
    seq = SEQ_AXES
    in_specs = (
        P(seq, DEV_AXES),
        P(seq, DEV_AXES),
        P(seq, DEV_AXES),
        P(seq, DEV_AXES),
        P(DEV_AXES),
        P(DEV_AXES, None, seq),
        P(DEV_AXES, None, seq),
        P(DEV_AXES, seq, None),
        P(seq + DEV_AXES, None),
        P(seq + DEV_AXES, None),
    )
    out_specs = P(seq + DEV_AXES, None)
    return jax.shard_map(
        per_device, mesh=fine, in_specs=in_specs, out_specs=out_specs, check_vma=False
    )
```

```python
import jax
import jax.numpy as jnp
import numpy as np
from jax import lax
from jax.sharding import Mesh
from jax.sharding import PartitionSpec as P

PAIR = 2

highest = lax.Precision.HIGHEST

SEQ_AXES = ("y", "xh", "xl", "c")
TOK_AXES = ("y", "xh")


def chain_join(earlier, later):
    scale = jnp.exp(later[:, -1:, :])
    state = scale * earlier[:, :-1, :] + later[:, :-1, :]
    return jnp.concatenate([state, earlier[:, -1:, :] + later[:, -1:, :]], axis=1)


def shifted(value, shift, count):
    pairs = [(i, i + shift) for i in range(count - shift)]
    return lax.ppermute(value, SEQ_AXES, pairs)


def carried_in(log_total, local_state, count):
    width = local_state.shape[-1]
    packed = jnp.concatenate(
        [local_state, jnp.broadcast_to(log_total[:, None, None], (log_total.shape[0], 1, width))],
        axis=1,
    )
    state = shifted(packed, 1, count)
    shift = 1
    while shift < count - 1:
        state = chain_join(shifted(state, shift, count), state)
        shift *= 2
    return state[:, :-1, :]


def head_norm(attention, gain):
    square_mean = jnp.mean(attention * attention, axis=-1, keepdims=True)
    return (attention * lax.rsqrt(square_mean + 1e-06) * gain).astype(jnp.bfloat16)


def slot_ranks(flat_experts, experts):
    onehot = (flat_experts[..., None] == jnp.arange(experts, dtype=jnp.int32)).astype(jnp.int32)
    before = jnp.cumsum(onehot, axis=-2) - onehot
    return jnp.sum(before * onehot, axis=-1)


def per_device(
    queries,
    key_vectors,
    value_vectors,
    log_decay,
    head_gain,
    gate_weight,
    up_weight,
    down_weight,
    expert_ids,
    expert_weights,
):
    count = 1
    for name in SEQ_AXES:
        count *= lax.axis_size(name)
    dev_count = lax.axis_size("dev")
    experts = dev_count // PAIR

    partner = [(0, 1), (1, 0)]
    gate_up = jnp.stack([gate_weight[0], up_weight[0]])
    gate_up = jnp.concatenate([gate_up, lax.ppermute(gate_up, "xl", partner)], axis=2)
    down_all = jnp.concatenate([down_weight[0], lax.ppermute(down_weight[0], "xl", partner)], axis=0)

    tok_count = expert_ids.shape[0]
    top_count = expert_ids.shape[1]
    capacity = max(2, (3 * tok_count * top_count + 2 * experts - 1) // (2 * experts))
    ids_all = lax.all_gather(expert_ids, "dev", axis=0, tiled=False)

    seq_len = queries.shape[0]
    heads = log_decay.shape[1]
    head_dim = queries.shape[1] // heads
    queries_h = jnp.transpose(queries.reshape(seq_len, heads, head_dim), (1, 0, 2))
    keys_h = jnp.transpose(key_vectors.reshape(seq_len, heads, head_dim), (1, 0, 2))
    values_h = jnp.transpose(value_vectors.reshape(seq_len, heads, head_dim), (1, 0, 2))
    decay_h = jnp.transpose(log_decay, (1, 0))
    running = jnp.cumsum(decay_h, axis=1)
    log_total = running[:, -1]
    tail_decay = jnp.exp(log_total[:, None] - running)
    keys_f = keys_h.astype(jnp.float32)
    values_f = values_h.astype(jnp.float32)
    local_state = jnp.einsum(
        "hsa,hsb->hab", keys_f * tail_decay[:, :, None], values_f, precision=highest
    )
    incoming = carried_in(log_total, local_state, count)

    causal = jnp.arange(seq_len)[:, None] >= jnp.arange(seq_len)[None, :]
    spread = jnp.where(causal[None], running[:, :, None] - running[:, None, :], 0.0)
    factors = jnp.where(causal[None], jnp.exp(spread), 0.0)
    scores = (
        jnp.einsum("hta,hsa->hts", queries_h, keys_h, preferred_element_type=jnp.float32) * factors
    )
    carried = jnp.exp(running)[:, :, None] * jnp.einsum(
        "hta,hab->htb", queries_h.astype(jnp.float32), incoming, precision=highest
    )
    attention = jnp.einsum("hts,hsb->htb", scores, values_f, precision=highest) + carried
    normed_h = head_norm(attention, head_gain.reshape(heads, 1, head_dim))
    normed = jnp.transpose(normed_h, (1, 0, 2)).reshape(seq_len, heads * head_dim)

    per_expert = dev_count * capacity
    flat = ids_all.reshape(dev_count, tok_count * top_count)
    rank = slot_ranks(flat, experts)
    source = jnp.arange(dev_count, dtype=jnp.int32)[:, None]
    slot_index = flat * per_expert + source * capacity + rank
    token_local = source * tok_count + jnp.arange(tok_count * top_count, dtype=jnp.int32)[None, :] // top_count
    slot_token = (
        jnp.full((experts * per_expert,), seq_len, jnp.int32)
        .at[slot_index.reshape(-1)]
        .set(token_local.reshape(-1))
    )
    padded = jnp.concatenate([normed, jnp.zeros((1, normed.shape[1]), normed.dtype)], axis=0)
    send_rows = jnp.repeat(padded[slot_token].reshape(experts, per_expert, -1), PAIR, axis=0)
    arrived = lax.all_to_all(send_rows, "dev", split_axis=0, concat_axis=0, tiled=True)
    local_rows = jnp.transpose(arrived.reshape(dev_count, per_expert, -1), (1, 0, 2)).reshape(
        per_expert, -1
    )
    width = local_rows.shape[1]
    gate_up = lax.all_gather(gate_up, "c", axis=2, tiled=True)
    down_all = lax.all_gather(down_all, "c", axis=0, tiled=True)
    groups = 1
    for name in TOK_AXES:
        groups *= lax.axis_size(name)
    piece = lax.all_to_all(
        jnp.broadcast_to(local_rows[None], (groups,) + local_rows.shape),
        TOK_AXES,
        split_axis=0,
        concat_axis=0,
        tiled=True,
    ).reshape(groups * per_expert, width)
    gate_part = jnp.dot(piece, gate_up[0], preferred_element_type=jnp.float32)
    up_part = jnp.dot(piece, gate_up[1], preferred_element_type=jnp.float32)
    hidden_all = (jax.nn.silu(gate_part) * up_part).astype(jnp.bfloat16)
    term = jnp.dot(hidden_all, down_all, preferred_element_type=jnp.float32).astype(jnp.bfloat16)
    parts = lax.all_to_all(
        term.reshape(groups, per_expert, width), TOK_AXES, split_axis=0, concat_axis=0, tiled=True
    )
    summed = jnp.sum(parts.astype(jnp.float32), axis=0).astype(jnp.bfloat16)
    returned = lax.all_to_all(
        summed.reshape(dev_count, capacity, width),
        "dev",
        split_axis=0,
        concat_axis=0,
        tiled=True,
    ).astype(jnp.float32)
    expert_out = jnp.sum(returned.reshape(experts, PAIR, capacity, width), axis=1).astype(
        jnp.bfloat16
    )
    own = lax.axis_index("dev")
    own_flat = lax.dynamic_index_in_dim(flat, own, 0, False)
    own_rank = lax.dynamic_index_in_dim(rank, own, 0, False)
    pick_index = own_flat * capacity + own_rank
    picked = expert_out.reshape(experts * capacity, width)[pick_index].reshape(
        tok_count, top_count, width
    )
    combined = jnp.sum(picked.astype(jnp.float32) * expert_weights[:, :, None], axis=1)
    return combined.astype(jnp.bfloat16)


def split_mesh(mesh):
    devices = mesh.devices
    seq_count, dev_count = devices.shape
    cores = 2
    xs = 4
    flat = devices.reshape(-1)
    if hasattr(flat[0], "coords"):
        cores = len({int(getattr(d, "core_on_chip", 0)) for d in flat})
        xs = len({int(d.coords[0]) for d in flat})
    ys = seq_count // (xs * cores)
    shape = (ys, xs // 2, 2, cores, dev_count)
    return Mesh(devices.reshape(shape), ("y", "xh", "xl", "c", "dev"))


def solution(mesh):
    fine = split_mesh(mesh)
    seq = SEQ_AXES
    in_specs = (
        P(seq, "dev"),
        P(seq, "dev"),
        P(seq, "dev"),
        P(seq, "dev"),
        P("dev"),
        P("dev", None, seq),
        P("dev", None, seq),
        P("dev", seq, None),
        P(seq + ("dev",), None),
        P(seq + ("dev",), None),
    )
    out_specs = P(seq + ("dev",), None)
    return jax.shard_map(
        per_device, mesh=fine, in_specs=in_specs, out_specs=out_specs, check_vma=False
    )
```

```python
import jax
import jax.numpy as jnp
import numpy as np
from jax import lax
from jax.sharding import Mesh
from jax.sharding import PartitionSpec as P

PAIR = 2

highest = lax.Precision.HIGHEST

SEQ_AXES = ("y", "xh", "xl", "c")
TOK_AXES = ("y", "xh")


def chain_join(earlier, later):
    scale = jnp.exp(later[:, -1:, :])
    state = scale * earlier[:, :-1, :] + later[:, :-1, :]
    return jnp.concatenate([state, earlier[:, -1:, :] + later[:, -1:, :]], axis=1)


def shifted(value, shift, count):
    pairs = [(i, i + shift) for i in range(count - shift)]
    return lax.ppermute(value, SEQ_AXES, pairs)


def carried_in(log_total, local_state, count):
    width = local_state.shape[-1]
    packed = jnp.concatenate(
        [local_state, jnp.broadcast_to(log_total[:, None, None], (log_total.shape[0], 1, width))],
        axis=1,
    )
    state = shifted(packed, 1, count)
    shift = 1
    while shift < count - 1:
        state = chain_join(shifted(state, shift, count), state)
        shift *= 2
    return state[:, :-1, :]


def head_norm(attention, gain):
    square_mean = jnp.mean(attention * attention, axis=-1, keepdims=True)
    return (attention * lax.rsqrt(square_mean + 1e-06) * gain).astype(jnp.bfloat16)


def slot_ranks(flat_experts, experts):
    onehot = (flat_experts[..., None] == jnp.arange(experts, dtype=jnp.int32)).astype(jnp.int32)
    before = jnp.cumsum(onehot, axis=-2) - onehot
    return jnp.sum(before * onehot, axis=-1)


def per_device(
    queries,
    key_vectors,
    value_vectors,
    log_decay,
    head_gain,
    gate_weight,
    up_weight,
    down_weight,
    expert_ids,
    expert_weights,
):
    count = 1
    for name in SEQ_AXES:
        count *= lax.axis_size(name)
    dev_count = lax.axis_size("dev")
    experts = dev_count // PAIR

    partner = [(0, 1), (1, 0)]
    gate_up = jnp.stack([gate_weight[0], up_weight[0]])
    gate_up = jnp.concatenate([gate_up, lax.ppermute(gate_up, "xl", partner)], axis=2)
    down_all = jnp.concatenate([down_weight[0], lax.ppermute(down_weight[0], "xl", partner)], axis=0)

    tok_count = expert_ids.shape[0]
    top_count = expert_ids.shape[1]
    capacity = max(2, (3 * tok_count * top_count + 2 * experts - 1) // (2 * experts))
    ids_all = lax.all_gather(expert_ids, "dev", axis=0, tiled=False)

    seq_len = queries.shape[0]
    heads = log_decay.shape[1]
    head_dim = queries.shape[1] // heads
    queries_h = jnp.transpose(queries.reshape(seq_len, heads, head_dim), (1, 0, 2))
    keys_h = jnp.transpose(key_vectors.reshape(seq_len, heads, head_dim), (1, 0, 2))
    values_h = jnp.transpose(value_vectors.reshape(seq_len, heads, head_dim), (1, 0, 2))
    decay_h = jnp.transpose(log_decay, (1, 0))
    running = jnp.cumsum(decay_h, axis=1)
    log_total = running[:, -1]
    tail_decay = jnp.exp(log_total[:, None] - running)
    keys_f = keys_h.astype(jnp.float32)
    values_f = values_h.astype(jnp.float32)
    local_state = jnp.einsum(
        "hsa,hsb->hab", keys_f * tail_decay[:, :, None], values_f, precision=highest
    )
    incoming = carried_in(log_total, local_state, count)

    causal = jnp.arange(seq_len)[:, None] >= jnp.arange(seq_len)[None, :]
    spread = jnp.where(causal[None], running[:, :, None] - running[:, None, :], 0.0)
    factors = jnp.where(causal[None], jnp.exp(spread), 0.0)
    scores = (
        jnp.einsum("hta,hsa->hts", queries_h, keys_h, preferred_element_type=jnp.float32) * factors
    )
    carried = jnp.exp(running)[:, :, None] * jnp.einsum(
        "hta,hab->htb", queries_h.astype(jnp.float32), incoming, precision=highest
    )
    attention = jnp.einsum("hts,hsb->htb", scores, values_f, precision=highest) + carried
    normed_h = head_norm(attention, head_gain.reshape(heads, 1, head_dim))
    normed = jnp.transpose(normed_h, (1, 0, 2)).reshape(seq_len, heads * head_dim)

    per_expert = dev_count * capacity
    flat = ids_all.reshape(dev_count, tok_count * top_count)
    rank = slot_ranks(flat, experts)
    source = jnp.arange(dev_count, dtype=jnp.int32)[:, None]
    slot_index = flat * per_expert + source * capacity + rank
    token_local = source * tok_count + jnp.arange(tok_count * top_count, dtype=jnp.int32)[None, :] // top_count
    slot_token = (
        jnp.full((experts * per_expert,), seq_len, jnp.int32)
        .at[slot_index.reshape(-1)]
        .set(token_local.reshape(-1))
    )
    padded = jnp.concatenate([normed, jnp.zeros((1, normed.shape[1]), normed.dtype)], axis=0)
    send_rows = jnp.repeat(padded[slot_token].reshape(experts, per_expert, -1), PAIR, axis=0)
    gate_up, down_all, send_rows = lax.optimization_barrier((gate_up, down_all, send_rows))
    gate_up = lax.all_gather(gate_up, "c", axis=2, tiled=True)
    down_all = lax.all_gather(down_all, "c", axis=0, tiled=True)
    arrived = lax.all_to_all(send_rows, "dev", split_axis=0, concat_axis=0, tiled=True)
    local_rows = jnp.transpose(arrived.reshape(dev_count, per_expert, -1), (1, 0, 2)).reshape(
        per_expert, -1
    )
    width = local_rows.shape[1]
    groups = 1
    for name in TOK_AXES:
        groups *= lax.axis_size(name)
    piece = lax.all_to_all(
        jnp.broadcast_to(local_rows[None], (groups,) + local_rows.shape),
        TOK_AXES,
        split_axis=0,
        concat_axis=0,
        tiled=True,
    ).reshape(groups * per_expert, width)
    gate_part = jnp.dot(piece, gate_up[0], preferred_element_type=jnp.float32)
    up_part = jnp.dot(piece, gate_up[1], preferred_element_type=jnp.float32)
    hidden_all = (jax.nn.silu(gate_part) * up_part).astype(jnp.bfloat16)
    term = jnp.dot(hidden_all, down_all, preferred_element_type=jnp.float32).astype(jnp.bfloat16)
    parts = lax.all_to_all(
        term.reshape(groups, per_expert, width), TOK_AXES, split_axis=0, concat_axis=0, tiled=True
    )
    summed = jnp.sum(parts.astype(jnp.float32), axis=0).astype(jnp.bfloat16)
    returned = lax.all_to_all(
        summed.reshape(dev_count, capacity, width),
        "dev",
        split_axis=0,
        concat_axis=0,
        tiled=True,
    ).astype(jnp.float32)
    expert_out = jnp.sum(returned.reshape(experts, PAIR, capacity, width), axis=1).astype(
        jnp.bfloat16
    )
    own = lax.axis_index("dev")
    own_flat = lax.dynamic_index_in_dim(flat, own, 0, False)
    own_rank = lax.dynamic_index_in_dim(rank, own, 0, False)
    pick_index = own_flat * capacity + own_rank
    picked = expert_out.reshape(experts * capacity, width)[pick_index].reshape(
        tok_count, top_count, width
    )
    combined = jnp.sum(picked.astype(jnp.float32) * expert_weights[:, :, None], axis=1)
    return combined.astype(jnp.bfloat16)


def split_mesh(mesh):
    devices = mesh.devices
    seq_count, dev_count = devices.shape
    cores = 2
    xs = 4
    flat = devices.reshape(-1)
    if hasattr(flat[0], "coords"):
        cores = len({int(getattr(d, "core_on_chip", 0)) for d in flat})
        xs = len({int(d.coords[0]) for d in flat})
    ys = seq_count // (xs * cores)
    shape = (ys, xs // 2, 2, cores, dev_count)
    return Mesh(devices.reshape(shape), ("y", "xh", "xl", "c", "dev"))


def solution(mesh):
    fine = split_mesh(mesh)
    seq = SEQ_AXES
    in_specs = (
        P(seq, "dev"),
        P(seq, "dev"),
        P(seq, "dev"),
        P(seq, "dev"),
        P("dev"),
        P("dev", None, seq),
        P("dev", None, seq),
        P("dev", seq, None),
        P(seq + ("dev",), None),
        P(seq + ("dev",), None),
    )
    out_specs = P(seq + ("dev",), None)
    return jax.shard_map(
        per_device, mesh=fine, in_specs=in_specs, out_specs=out_specs, check_vma=False
    )
```

```python
import jax
import jax.numpy as jnp
import numpy as np
from jax import lax
from jax.sharding import Mesh
from jax.sharding import PartitionSpec as P

PAIR = 2

highest = lax.Precision.HIGHEST

SEQ_AXES = ("y", "xh", "xl", "c")
TOK_AXES = ("y", "xh")
ROUTE_AXES = ("y", "xh", "dev")


def chain_join(earlier, later):
    scale = jnp.exp(later[:, -1:, :])
    state = scale * earlier[:, :-1, :] + later[:, :-1, :]
    return jnp.concatenate([state, earlier[:, -1:, :] + later[:, -1:, :]], axis=1)


def shifted(value, shift, count):
    pairs = [(i, i + shift) for i in range(count - shift)]
    return lax.ppermute(value, SEQ_AXES, pairs)


def carried_in(log_total, local_state, count):
    width = local_state.shape[-1]
    packed = jnp.concatenate(
        [local_state, jnp.broadcast_to(log_total[:, None, None], (log_total.shape[0], 1, width))],
        axis=1,
    )
    state = shifted(packed, 1, count)
    shift = 1
    while shift < count - 1:
        state = chain_join(shifted(state, shift, count), state)
        shift *= 2
    return state[:, :-1, :]


def head_norm(attention, gain):
    square_mean = jnp.mean(attention * attention, axis=-1, keepdims=True)
    return (attention * lax.rsqrt(square_mean + 1e-06) * gain).astype(jnp.bfloat16)


def slot_ranks(flat_experts, experts):
    onehot = (flat_experts[..., None] == jnp.arange(experts, dtype=jnp.int32)).astype(jnp.int32)
    before = jnp.cumsum(onehot, axis=-2) - onehot
    return jnp.sum(before * onehot, axis=-1)


def per_device(
    queries,
    key_vectors,
    value_vectors,
    log_decay,
    head_gain,
    gate_weight,
    up_weight,
    down_weight,
    expert_ids,
    expert_weights,
):
    count = 1
    for name in SEQ_AXES:
        count *= lax.axis_size(name)
    dev_count = lax.axis_size("dev")
    experts = dev_count // PAIR

    partner = [(0, 1), (1, 0)]
    gate_up = jnp.stack([gate_weight[0], up_weight[0]])
    gate_up = jnp.concatenate([gate_up, lax.ppermute(gate_up, "xl", partner)], axis=2)
    down_all = jnp.concatenate([down_weight[0], lax.ppermute(down_weight[0], "xl", partner)], axis=0)
    gate_up = lax.all_gather(gate_up, "c", axis=2, tiled=True)
    down_all = lax.all_gather(down_all, "c", axis=0, tiled=True)

    tok_count = expert_ids.shape[0]
    top_count = expert_ids.shape[1]
    capacity = max(2, (3 * tok_count * top_count + 2 * experts - 1) // (2 * experts))
    ids_all = lax.all_gather(expert_ids, "dev", axis=0, tiled=False)

    seq_len = queries.shape[0]
    heads = log_decay.shape[1]
    head_dim = queries.shape[1] // heads
    queries_h = jnp.transpose(queries.reshape(seq_len, heads, head_dim), (1, 0, 2))
    keys_h = jnp.transpose(key_vectors.reshape(seq_len, heads, head_dim), (1, 0, 2))
    values_h = jnp.transpose(value_vectors.reshape(seq_len, heads, head_dim), (1, 0, 2))
    decay_h = jnp.transpose(log_decay, (1, 0))
    running = jnp.cumsum(decay_h, axis=1)
    log_total = running[:, -1]
    tail_decay = jnp.exp(log_total[:, None] - running)
    keys_f = keys_h.astype(jnp.float32)
    values_f = values_h.astype(jnp.float32)
    local_state = jnp.einsum(
        "hsa,hsb->hab", keys_f * tail_decay[:, :, None], values_f, precision=highest
    )
    incoming = carried_in(log_total, local_state, count)

    causal = jnp.arange(seq_len)[:, None] >= jnp.arange(seq_len)[None, :]
    spread = jnp.where(causal[None], running[:, :, None] - running[:, None, :], 0.0)
    factors = jnp.where(causal[None], jnp.exp(spread), 0.0)
    scores = (
        jnp.einsum("hta,hsa->hts", queries_h, keys_h, preferred_element_type=jnp.float32) * factors
    )
    carried = jnp.exp(running)[:, :, None] * jnp.einsum(
        "hta,hab->htb", queries_h.astype(jnp.float32), incoming, precision=highest
    )
    attention = jnp.einsum("hts,hsb->htb", scores, values_f, precision=highest) + carried
    normed_h = head_norm(attention, head_gain.reshape(heads, 1, head_dim))
    normed = jnp.transpose(normed_h, (1, 0, 2)).reshape(seq_len, heads * head_dim)

    per_expert = dev_count * capacity
    flat = ids_all.reshape(dev_count, tok_count * top_count)
    rank = slot_ranks(flat, experts)
    source = jnp.arange(dev_count, dtype=jnp.int32)[:, None]
    slot_index = flat * per_expert + source * capacity + rank
    token_local = source * tok_count + jnp.arange(tok_count * top_count, dtype=jnp.int32)[None, :] // top_count
    slot_token = (
        jnp.full((experts * per_expert,), seq_len, jnp.int32)
        .at[slot_index.reshape(-1)]
        .set(token_local.reshape(-1))
    )
    padded = jnp.concatenate([normed, jnp.zeros((1, normed.shape[1]), normed.dtype)], axis=0)
    groups = 1
    for name in TOK_AXES:
        groups *= lax.axis_size(name)
    send_rows = jnp.repeat(padded[slot_token].reshape(experts, per_expert, -1), PAIR, axis=0)
    send_rows = jnp.broadcast_to(send_rows[None], (groups,) + send_rows.shape)
    arrived = lax.all_to_all(
        send_rows.reshape((groups * dev_count,) + send_rows.shape[2:]),
        ROUTE_AXES,
        split_axis=0,
        concat_axis=0,
        tiled=True,
    )
    head_width = arrived.shape[-1]
    piece = jnp.transpose(
        arrived.reshape(groups, dev_count, per_expert, head_width), (0, 2, 1, 3)
    ).reshape(groups * per_expert, dev_count * head_width)
    width = piece.shape[1]
    gate_part = jnp.dot(piece, gate_up[0], preferred_element_type=jnp.float32)
    up_part = jnp.dot(piece, gate_up[1], preferred_element_type=jnp.float32)
    hidden_all = (jax.nn.silu(gate_part) * up_part).astype(jnp.bfloat16)
    term = jnp.dot(hidden_all, down_all, preferred_element_type=jnp.float32).astype(jnp.bfloat16)
    parts = lax.all_to_all(
        term.reshape(groups * dev_count, capacity, width),
        ROUTE_AXES,
        split_axis=0,
        concat_axis=0,
        tiled=True,
    ).astype(jnp.float32)
    expert_out = jnp.sum(
        parts.reshape(groups, experts, PAIR, capacity, width), axis=(0, 2)
    ).astype(jnp.bfloat16)
    own = lax.axis_index("dev")
    own_flat = lax.dynamic_index_in_dim(flat, own, 0, False)
    own_rank = lax.dynamic_index_in_dim(rank, own, 0, False)
    pick_index = own_flat * capacity + own_rank
    picked = expert_out.reshape(experts * capacity, width)[pick_index].reshape(
        tok_count, top_count, width
    )
    combined = jnp.sum(picked.astype(jnp.float32) * expert_weights[:, :, None], axis=1)
    return combined.astype(jnp.bfloat16)


def split_mesh(mesh):
    devices = mesh.devices
    seq_count, dev_count = devices.shape
    cores = 2
    xs = 4
    flat = devices.reshape(-1)
    if hasattr(flat[0], "coords"):
        cores = len({int(getattr(d, "core_on_chip", 0)) for d in flat})
        xs = len({int(d.coords[0]) for d in flat})
    ys = seq_count // (xs * cores)
    shape = (ys, xs // 2, 2, cores, dev_count)
    return Mesh(devices.reshape(shape), ("y", "xh", "xl", "c", "dev"))


def solution(mesh):
    fine = split_mesh(mesh)
    seq = SEQ_AXES
    in_specs = (
        P(seq, "dev"),
        P(seq, "dev"),
        P(seq, "dev"),
        P(seq, "dev"),
        P("dev"),
        P("dev", None, seq),
        P("dev", None, seq),
        P("dev", seq, None),
        P(seq + ("dev",), None),
        P(seq + ("dev",), None),
    )
    out_specs = P(seq + ("dev",), None)
    return jax.shard_map(
        per_device, mesh=fine, in_specs=in_specs, out_specs=out_specs, check_vma=False
    )
```

```python
import jax
import jax.numpy as jnp
import numpy as np
from jax import lax
from jax.sharding import Mesh
from jax.sharding import PartitionSpec as P

PAIR = 2

highest = lax.Precision.HIGHEST

SEQ_AXES = ("y", "xh", "xl", "c")
TOK_AXES = ("y", "xh")


def chain_join(earlier, later):
    scale = jnp.exp(later[:, -1:, :])
    state = scale * earlier[:, :-1, :] + later[:, :-1, :]
    return jnp.concatenate([state, earlier[:, -1:, :] + later[:, -1:, :]], axis=1)


def shifted(value, shift, count):
    pairs = [(i, i + shift) for i in range(count - shift)]
    return lax.ppermute(value, SEQ_AXES, pairs)


def carried_in(log_total, local_state, count):
    width = local_state.shape[-1]
    packed = jnp.concatenate(
        [local_state, jnp.broadcast_to(log_total[:, None, None], (log_total.shape[0], 1, width))],
        axis=1,
    )
    state = shifted(packed, 1, count)
    shift = 1
    while shift < count - 1:
        state = chain_join(shifted(state, shift, count), state)
        shift *= 2
    return state[:, :-1, :]


def head_norm(attention, gain):
    square_mean = jnp.mean(attention * attention, axis=-1, keepdims=True)
    return (attention * lax.rsqrt(square_mean + 1e-06) * gain).astype(jnp.bfloat16)


def slot_ranks(flat_experts, experts):
    onehot = (flat_experts[..., None] == jnp.arange(experts, dtype=jnp.int32)).astype(jnp.int32)
    before = jnp.cumsum(onehot, axis=-2) - onehot
    return jnp.sum(before * onehot, axis=-1)


def per_device(
    queries,
    key_vectors,
    value_vectors,
    log_decay,
    head_gain,
    gate_weight,
    up_weight,
    down_weight,
    expert_ids,
    expert_weights,
):
    count = 1
    for name in SEQ_AXES:
        count *= lax.axis_size(name)
    dev_count = lax.axis_size("dev")
    experts = dev_count // PAIR

    partner = [(0, 1), (1, 0)]
    gate_up = jnp.stack([gate_weight[0], up_weight[0]])
    gate_up = jnp.concatenate([gate_up, lax.ppermute(gate_up, "xl", partner)], axis=2)
    down_all = jnp.concatenate([down_weight[0], lax.ppermute(down_weight[0], "xl", partner)], axis=0)

    tok_count = expert_ids.shape[0]
    top_count = expert_ids.shape[1]
    capacity = max(2, (3 * tok_count * top_count + 2 * experts - 1) // (2 * experts))
    ids_all = lax.all_gather(expert_ids, "dev", axis=0, tiled=False)
    gate_up, down_all, ids_all = lax.optimization_barrier((gate_up, down_all, ids_all))

    seq_len = queries.shape[0]
    heads = log_decay.shape[1]
    head_dim = queries.shape[1] // heads
    queries_h = jnp.transpose(queries.reshape(seq_len, heads, head_dim), (1, 0, 2))
    keys_h = jnp.transpose(key_vectors.reshape(seq_len, heads, head_dim), (1, 0, 2))
    values_h = jnp.transpose(value_vectors.reshape(seq_len, heads, head_dim), (1, 0, 2))
    decay_h = jnp.transpose(log_decay, (1, 0))
    running = jnp.cumsum(decay_h, axis=1)
    log_total = running[:, -1]
    tail_decay = jnp.exp(log_total[:, None] - running)
    keys_f = keys_h.astype(jnp.float32)
    values_f = values_h.astype(jnp.float32)
    local_state = jnp.einsum(
        "hsa,hsb->hab", keys_f * tail_decay[:, :, None], values_f, precision=highest
    )
    incoming = carried_in(log_total, local_state, count)

    causal = jnp.arange(seq_len)[:, None] >= jnp.arange(seq_len)[None, :]
    spread = jnp.where(causal[None], running[:, :, None] - running[:, None, :], 0.0)
    factors = jnp.where(causal[None], jnp.exp(spread), 0.0)
    scores = (
        jnp.einsum("hta,hsa->hts", queries_h, keys_h, preferred_element_type=jnp.float32) * factors
    )
    carried = jnp.exp(running)[:, :, None] * jnp.einsum(
        "hta,hab->htb", queries_h.astype(jnp.float32), incoming, precision=highest
    )
    attention = jnp.einsum("hts,hsb->htb", scores, values_f, precision=highest) + carried
    normed_h = head_norm(attention, head_gain.reshape(heads, 1, head_dim))
    normed = jnp.transpose(normed_h, (1, 0, 2)).reshape(seq_len, heads * head_dim)

    per_expert = dev_count * capacity
    flat = ids_all.reshape(dev_count, tok_count * top_count)
    rank = slot_ranks(flat, experts)
    source = jnp.arange(dev_count, dtype=jnp.int32)[:, None]
    slot_index = flat * per_expert + source * capacity + rank
    token_local = source * tok_count + jnp.arange(tok_count * top_count, dtype=jnp.int32)[None, :] // top_count
    slot_token = (
        jnp.full((experts * per_expert,), seq_len, jnp.int32)
        .at[slot_index.reshape(-1)]
        .set(token_local.reshape(-1))
    )
    padded = jnp.concatenate([normed, jnp.zeros((1, normed.shape[1]), normed.dtype)], axis=0)
    send_rows = jnp.repeat(padded[slot_token].reshape(experts, per_expert, -1), PAIR, axis=0)
    arrived = lax.all_to_all(send_rows, "dev", split_axis=0, concat_axis=0, tiled=True)
    local_rows = jnp.transpose(arrived.reshape(dev_count, per_expert, -1), (1, 0, 2)).reshape(
        per_expert, -1
    )
    width = local_rows.shape[1]
    gate_up = lax.all_gather(gate_up, "c", axis=2, tiled=True)
    down_all = lax.all_gather(down_all, "c", axis=0, tiled=True)
    groups = 1
    for name in TOK_AXES:
        groups *= lax.axis_size(name)
    piece = lax.all_to_all(
        jnp.broadcast_to(local_rows[None], (groups,) + local_rows.shape),
        TOK_AXES,
        split_axis=0,
        concat_axis=0,
        tiled=True,
    ).reshape(groups * per_expert, width)
    gate_part = jnp.dot(piece, gate_up[0], preferred_element_type=jnp.float32)
    up_part = jnp.dot(piece, gate_up[1], preferred_element_type=jnp.float32)
    hidden_all = (jax.nn.silu(gate_part) * up_part).astype(jnp.bfloat16)
    term = jnp.dot(hidden_all, down_all, preferred_element_type=jnp.float32).astype(jnp.bfloat16)
    parts = lax.all_to_all(
        term.reshape(groups, per_expert, width), TOK_AXES, split_axis=0, concat_axis=0, tiled=True
    )
    summed = jnp.sum(parts.astype(jnp.float32), axis=0).astype(jnp.bfloat16)
    returned = lax.all_to_all(
        summed.reshape(dev_count, capacity, width),
        "dev",
        split_axis=0,
        concat_axis=0,
        tiled=True,
    ).astype(jnp.float32)
    expert_out = jnp.sum(returned.reshape(experts, PAIR, capacity, width), axis=1).astype(
        jnp.bfloat16
    )
    own = lax.axis_index("dev")
    own_flat = lax.dynamic_index_in_dim(flat, own, 0, False)
    own_rank = lax.dynamic_index_in_dim(rank, own, 0, False)
    pick_index = own_flat * capacity + own_rank
    picked = expert_out.reshape(experts * capacity, width)[pick_index].reshape(
        tok_count, top_count, width
    )
    combined = jnp.sum(picked.astype(jnp.float32) * expert_weights[:, :, None], axis=1)
    return combined.astype(jnp.bfloat16)


def split_mesh(mesh):
    devices = mesh.devices
    seq_count, dev_count = devices.shape
    cores = 2
    xs = 4
    flat = devices.reshape(-1)
    if hasattr(flat[0], "coords"):
        cores = len({int(getattr(d, "core_on_chip", 0)) for d in flat})
        xs = len({int(d.coords[0]) for d in flat})
    ys = seq_count // (xs * cores)
    shape = (ys, xs // 2, 2, cores, dev_count)
    return Mesh(devices.reshape(shape), ("y", "xh", "xl", "c", "dev"))


def solution(mesh):
    fine = split_mesh(mesh)
    seq = SEQ_AXES
    in_specs = (
        P(seq, "dev"),
        P(seq, "dev"),
        P(seq, "dev"),
        P(seq, "dev"),
        P("dev"),
        P("dev", None, seq),
        P("dev", None, seq),
        P("dev", seq, None),
        P(seq + ("dev",), None),
        P(seq + ("dev",), None),
    )
    out_specs = P(seq + ("dev",), None)
    return jax.shard_map(
        per_device, mesh=fine, in_specs=in_specs, out_specs=out_specs, check_vma=False
    )
```

```python
import jax
import jax.numpy as jnp
import numpy as np
from jax import lax
from jax.sharding import Mesh
from jax.sharding import PartitionSpec as P

PAIR = 2

highest = lax.Precision.HIGHEST

SEQ_AXES = ("y", "x", "c")
TOK_AXES = ("y", "x")
DEV_AXES = ("e", "p")


def chain_join(earlier, later):
    scale = jnp.exp(later[:, -1:, :])
    state = scale * earlier[:, :-1, :] + later[:, :-1, :]
    return jnp.concatenate([state, earlier[:, -1:, :] + later[:, -1:, :]], axis=1)


def shifted(value, shift, count):
    pairs = [(i, i + shift) for i in range(count - shift)]
    return lax.ppermute(value, SEQ_AXES, pairs)


def carried_in(log_total, local_state, count):
    width = local_state.shape[-1]
    packed = jnp.concatenate(
        [local_state, jnp.broadcast_to(log_total[:, None, None], (log_total.shape[0], 1, width))],
        axis=1,
    )
    state = shifted(packed, 1, count)
    shift = 1
    while shift < count - 1:
        state = chain_join(shifted(state, shift, count), state)
        shift *= 2
    return state[:, :-1, :]


def head_norm(attention, gain):
    square_mean = jnp.mean(attention * attention, axis=-1, keepdims=True)
    return (attention * lax.rsqrt(square_mean + 1e-06) * gain).astype(jnp.bfloat16)


def slot_ranks(flat_experts, experts):
    onehot = (flat_experts[..., None] == jnp.arange(experts, dtype=jnp.int32)).astype(jnp.int32)
    before = jnp.cumsum(onehot, axis=-2) - onehot
    return jnp.sum(before * onehot, axis=-1)


def per_device(
    queries,
    key_vectors,
    value_vectors,
    log_decay,
    head_gain,
    gate_weight,
    up_weight,
    down_weight,
    expert_ids,
    expert_weights,
):
    count = 1
    for name in SEQ_AXES:
        count *= lax.axis_size(name)
    dev_count = lax.axis_size("e") * lax.axis_size("p")
    experts = dev_count // PAIR

    ids_all = lax.all_gather(expert_ids, DEV_AXES, axis=0, tiled=False)
    partner = [(0, 1), (1, 0)]
    gate_up = jnp.stack([gate_weight[0], up_weight[0]])
    gate_up, down_own, ids_all = lax.optimization_barrier((gate_up, down_weight[0], ids_all))
    gate_up = jnp.concatenate([gate_up, lax.ppermute(gate_up, "p", partner)], axis=2)
    down_all = jnp.concatenate([down_own, lax.ppermute(down_own, "p", partner)], axis=0)

    tok_count = expert_ids.shape[0]
    top_count = expert_ids.shape[1]
    capacity = max(2, (3 * tok_count * top_count + 2 * experts - 1) // (2 * experts))
    capacity = -(-capacity // PAIR) * PAIR
    half = capacity // PAIR

    seq_len = queries.shape[0]
    heads = log_decay.shape[1]
    head_dim = queries.shape[1] // heads
    queries_h = jnp.transpose(queries.reshape(seq_len, heads, head_dim), (1, 0, 2))
    keys_h = jnp.transpose(key_vectors.reshape(seq_len, heads, head_dim), (1, 0, 2))
    values_h = jnp.transpose(value_vectors.reshape(seq_len, heads, head_dim), (1, 0, 2))
    decay_h = jnp.transpose(log_decay, (1, 0))
    running = jnp.cumsum(decay_h, axis=1)
    log_total = running[:, -1]
    tail_decay = jnp.exp(log_total[:, None] - running)
    keys_f = keys_h.astype(jnp.float32)
    values_f = values_h.astype(jnp.float32)
    local_state = jnp.einsum(
        "hsa,hsb->hab", keys_f * tail_decay[:, :, None], values_f, precision=highest
    )
    incoming = carried_in(log_total, local_state, count)

    causal = jnp.arange(seq_len)[:, None] >= jnp.arange(seq_len)[None, :]
    spread = jnp.where(causal[None], running[:, :, None] - running[:, None, :], 0.0)
    factors = jnp.where(causal[None], jnp.exp(spread), 0.0)
    scores = (
        jnp.einsum("hta,hsa->hts", queries_h, keys_h, preferred_element_type=jnp.float32) * factors
    )
    carried = jnp.exp(running)[:, :, None] * jnp.einsum(
        "hta,hab->htb", queries_h.astype(jnp.float32), incoming, precision=highest
    )
    attention = jnp.einsum("hts,hsb->htb", scores, values_f, precision=highest) + carried
    normed_h = head_norm(attention, head_gain.reshape(heads, 1, head_dim))
    normed = jnp.transpose(normed_h, (1, 0, 2)).reshape(seq_len, heads * head_dim)

    per_dev = dev_count * half
    flat = ids_all.reshape(dev_count, tok_count * top_count)
    rank = slot_ranks(flat, experts)
    source = jnp.arange(dev_count, dtype=jnp.int32)[:, None]
    slot_index = (flat * PAIR + rank // half) * per_dev + source * half + rank % half
    token_local = source * tok_count + jnp.arange(tok_count * top_count, dtype=jnp.int32)[None, :] // top_count
    slot_token = (
        jnp.full((dev_count * per_dev,), seq_len, jnp.int32)
        .at[slot_index.reshape(-1)]
        .set(token_local.reshape(-1))
    )
    padded = jnp.concatenate([normed, jnp.zeros((1, normed.shape[1]), normed.dtype)], axis=0)
    send_rows = padded[slot_token].reshape(dev_count, per_dev, -1)
    gate_up, down_all, send_rows = lax.optimization_barrier((gate_up, down_all, send_rows))
    gate_up = lax.all_gather(gate_up, "c", axis=2, tiled=True)
    down_all = lax.all_gather(down_all, "c", axis=0, tiled=True)
    arrived = lax.all_to_all(send_rows, DEV_AXES, split_axis=0, concat_axis=0, tiled=True)
    local_rows = jnp.transpose(arrived, (1, 0, 2)).reshape(per_dev, -1)
    width = local_rows.shape[1]
    groups = 1
    for name in TOK_AXES:
        groups *= lax.axis_size(name)
    piece = lax.all_to_all(
        jnp.broadcast_to(local_rows[None], (groups,) + local_rows.shape),
        TOK_AXES,
        split_axis=0,
        concat_axis=0,
        tiled=True,
    ).reshape(groups * per_dev, width)
    gate_part = jnp.dot(piece, gate_up[0], preferred_element_type=jnp.float32)
    up_part = jnp.dot(piece, gate_up[1], preferred_element_type=jnp.float32)
    hidden_all = (jax.nn.silu(gate_part) * up_part).astype(jnp.bfloat16)
    term = jnp.dot(hidden_all, down_all, preferred_element_type=jnp.float32).astype(jnp.bfloat16)
    parts = lax.all_to_all(
        term.reshape(groups, per_dev, width), TOK_AXES, split_axis=0, concat_axis=0, tiled=True
    )
    summed = jnp.sum(parts.astype(jnp.float32), axis=0).astype(jnp.bfloat16)
    returned = lax.all_to_all(
        summed.reshape(dev_count, half, width),
        DEV_AXES,
        split_axis=0,
        concat_axis=0,
        tiled=True,
    )
    own = lax.axis_index(DEV_AXES)
    own_flat = lax.dynamic_index_in_dim(flat, own, 0, False)
    own_rank = lax.dynamic_index_in_dim(rank, own, 0, False)
    pick_index = own_flat * capacity + own_rank
    picked = returned.reshape(dev_count * half, width)[pick_index].reshape(
        tok_count, top_count, width
    )
    combined = jnp.sum(picked.astype(jnp.float32) * expert_weights[:, :, None], axis=1)
    return combined.astype(jnp.bfloat16)


def split_mesh(mesh):
    devices = mesh.devices
    seq_count, dev_count = devices.shape
    cores = 2
    xs = 4
    flat = devices.reshape(-1)
    if hasattr(flat[0], "coords"):
        cores = len({int(getattr(d, "core_on_chip", 0)) for d in flat})
        xs = len({int(d.coords[0]) for d in flat})
    ys = seq_count // (xs * cores)
    shape = (ys, xs, cores, dev_count // PAIR, PAIR)
    return Mesh(devices.reshape(shape), ("y", "x", "c", "e", "p"))


def solution(mesh):
    fine = split_mesh(mesh)
    seq = SEQ_AXES
    in_specs = (
        P(seq, DEV_AXES),
        P(seq, DEV_AXES),
        P(seq, DEV_AXES),
        P(seq, DEV_AXES),
        P(DEV_AXES),
        P(DEV_AXES, None, seq),
        P(DEV_AXES, None, seq),
        P(DEV_AXES, seq, None),
        P(seq + DEV_AXES, None),
        P(seq + DEV_AXES, None),
    )
    out_specs = P(seq + DEV_AXES, None)
    return jax.shard_map(
        per_device, mesh=fine, in_specs=in_specs, out_specs=out_specs, check_vma=False
    )
```

```python
import jax
import jax.numpy as jnp
import numpy as np
from jax import lax
from jax.sharding import Mesh
from jax.sharding import PartitionSpec as P

PAIR = 2

highest = lax.Precision.HIGHEST

SEQ_AXES = ("y", "x", "c")
TOK_AXES = ("y", "x")
DEV_AXES = ("e", "p")


def chain_join(earlier, later):
    scale = jnp.exp(later[:, -1:, :])
    state = scale * earlier[:, :-1, :] + later[:, :-1, :]
    return jnp.concatenate([state, earlier[:, -1:, :] + later[:, -1:, :]], axis=1)


def shifted(value, shift, count):
    pairs = [(i, i + shift) for i in range(count - shift)]
    return lax.ppermute(value, SEQ_AXES, pairs)


def carried_in(log_total, local_state, count):
    width = local_state.shape[-1]
    window = jnp.concatenate(
        [local_state, jnp.broadcast_to(log_total[:, None, None], (log_total.shape[0], 1, width))],
        axis=1,
    )
    earlier = None
    shift = 1
    while shift < count:
        arrived = shifted(window, shift, count)
        earlier = arrived if earlier is None else chain_join(arrived, earlier)
        if 2 * shift < count:
            window = chain_join(arrived, window)
        shift *= 2
    return earlier[:, :-1, :]


def head_norm(attention, gain):
    square_mean = jnp.mean(attention * attention, axis=-1, keepdims=True)
    return (attention * lax.rsqrt(square_mean + 1e-06) * gain).astype(jnp.bfloat16)


def slot_ranks(flat_experts, experts):
    onehot = (flat_experts[..., None] == jnp.arange(experts, dtype=jnp.int32)).astype(jnp.int32)
    before = jnp.cumsum(onehot, axis=-2) - onehot
    return jnp.sum(before * onehot, axis=-1)


def per_device(
    queries,
    key_vectors,
    value_vectors,
    log_decay,
    head_gain,
    gate_weight,
    up_weight,
    down_weight,
    expert_ids,
    expert_weights,
):
    count = 1
    for name in SEQ_AXES:
        count *= lax.axis_size(name)
    dev_count = lax.axis_size("e") * lax.axis_size("p")
    experts = dev_count // PAIR

    ids_all = lax.all_gather(expert_ids, DEV_AXES, axis=0, tiled=False)
    partner = [(0, 1), (1, 0)]
    gate_up = jnp.stack([gate_weight[0], up_weight[0]])
    gate_up, down_own, ids_all = lax.optimization_barrier((gate_up, down_weight[0], ids_all))
    gate_up = jnp.concatenate([gate_up, lax.ppermute(gate_up, "p", partner)], axis=2)
    down_all = jnp.concatenate([down_own, lax.ppermute(down_own, "p", partner)], axis=0)

    tok_count = expert_ids.shape[0]
    top_count = expert_ids.shape[1]
    capacity = max(2, (3 * tok_count * top_count + 2 * experts - 1) // (2 * experts))
    capacity = -(-capacity // PAIR) * PAIR
    half = capacity // PAIR

    seq_len = queries.shape[0]
    heads = log_decay.shape[1]
    head_dim = queries.shape[1] // heads
    queries_h = jnp.transpose(queries.reshape(seq_len, heads, head_dim), (1, 0, 2))
    keys_h = jnp.transpose(key_vectors.reshape(seq_len, heads, head_dim), (1, 0, 2))
    values_h = jnp.transpose(value_vectors.reshape(seq_len, heads, head_dim), (1, 0, 2))
    decay_h = jnp.transpose(log_decay, (1, 0))
    running = jnp.cumsum(decay_h, axis=1)
    log_total = running[:, -1]
    tail_decay = jnp.exp(log_total[:, None] - running)
    keys_f = keys_h.astype(jnp.float32)
    values_f = values_h.astype(jnp.float32)
    local_state = jnp.einsum(
        "hsa,hsb->hab", keys_f * tail_decay[:, :, None], values_f, precision=highest
    )
    incoming = carried_in(log_total, local_state, count)

    causal = jnp.arange(seq_len)[:, None] >= jnp.arange(seq_len)[None, :]
    spread = jnp.where(causal[None], running[:, :, None] - running[:, None, :], 0.0)
    factors = jnp.where(causal[None], jnp.exp(spread), 0.0)
    scores = (
        jnp.einsum("hta,hsa->hts", queries_h, keys_h, preferred_element_type=jnp.float32) * factors
    )
    carried = jnp.exp(running)[:, :, None] * jnp.einsum(
        "hta,hab->htb", queries_h.astype(jnp.float32), incoming, precision=highest
    )
    attention = jnp.einsum("hts,hsb->htb", scores, values_f, precision=highest) + carried
    normed_h = head_norm(attention, head_gain.reshape(heads, 1, head_dim))
    normed = jnp.transpose(normed_h, (1, 0, 2)).reshape(seq_len, heads * head_dim)

    per_dev = dev_count * half
    flat = ids_all.reshape(dev_count, tok_count * top_count)
    rank = slot_ranks(flat, experts)
    source = jnp.arange(dev_count, dtype=jnp.int32)[:, None]
    slot_index = (flat * PAIR + rank // half) * per_dev + source * half + rank % half
    token_local = source * tok_count + jnp.arange(tok_count * top_count, dtype=jnp.int32)[None, :] // top_count
    slot_token = (
        jnp.full((dev_count * per_dev,), seq_len, jnp.int32)
        .at[slot_index.reshape(-1)]
        .set(token_local.reshape(-1))
    )
    padded = jnp.concatenate([normed, jnp.zeros((1, normed.shape[1]), normed.dtype)], axis=0)
    send_rows = padded[slot_token].reshape(dev_count, per_dev, -1)
    gate_up, down_all, send_rows = lax.optimization_barrier((gate_up, down_all, send_rows))
    gate_up = lax.all_gather(gate_up, "c", axis=2, tiled=True)
    down_all = lax.all_gather(down_all, "c", axis=0, tiled=True)
    arrived = lax.all_to_all(send_rows, DEV_AXES, split_axis=0, concat_axis=0, tiled=True)
    local_rows = jnp.transpose(arrived, (1, 0, 2)).reshape(per_dev, -1)
    width = local_rows.shape[1]
    groups = 1
    for name in TOK_AXES:
        groups *= lax.axis_size(name)
    piece = lax.all_to_all(
        jnp.broadcast_to(local_rows[None], (groups,) + local_rows.shape),
        TOK_AXES,
        split_axis=0,
        concat_axis=0,
        tiled=True,
    ).reshape(groups * per_dev, width)
    gate_part = jnp.dot(piece, gate_up[0], preferred_element_type=jnp.float32)
    up_part = jnp.dot(piece, gate_up[1], preferred_element_type=jnp.float32)
    hidden_all = (jax.nn.silu(gate_part) * up_part).astype(jnp.bfloat16)
    term = jnp.dot(hidden_all, down_all, preferred_element_type=jnp.float32).astype(jnp.bfloat16)
    parts = lax.all_to_all(
        term.reshape(groups, per_dev, width), TOK_AXES, split_axis=0, concat_axis=0, tiled=True
    )
    summed = jnp.sum(parts.astype(jnp.float32), axis=0).astype(jnp.bfloat16)
    returned = lax.all_to_all(
        summed.reshape(dev_count, half, width),
        DEV_AXES,
        split_axis=0,
        concat_axis=0,
        tiled=True,
    )
    own = lax.axis_index(DEV_AXES)
    own_flat = lax.dynamic_index_in_dim(flat, own, 0, False)
    own_rank = lax.dynamic_index_in_dim(rank, own, 0, False)
    pick_index = own_flat * capacity + own_rank
    picked = returned.reshape(dev_count * half, width)[pick_index].reshape(
        tok_count, top_count, width
    )
    combined = jnp.sum(picked.astype(jnp.float32) * expert_weights[:, :, None], axis=1)
    return combined.astype(jnp.bfloat16)


def split_mesh(mesh):
    devices = mesh.devices
    seq_count, dev_count = devices.shape
    cores = 2
    xs = 4
    flat = devices.reshape(-1)
    if hasattr(flat[0], "coords"):
        cores = len({int(getattr(d, "core_on_chip", 0)) for d in flat})
        xs = len({int(d.coords[0]) for d in flat})
    ys = seq_count // (xs * cores)
    shape = (ys, xs, cores, dev_count // PAIR, PAIR)
    return Mesh(devices.reshape(shape), ("y", "x", "c", "e", "p"))


def solution(mesh):
    fine = split_mesh(mesh)
    seq = SEQ_AXES
    in_specs = (
        P(seq, DEV_AXES),
        P(seq, DEV_AXES),
        P(seq, DEV_AXES),
        P(seq, DEV_AXES),
        P(DEV_AXES),
        P(DEV_AXES, None, seq),
        P(DEV_AXES, None, seq),
        P(DEV_AXES, seq, None),
        P(seq + DEV_AXES, None),
        P(seq + DEV_AXES, None),
    )
    out_specs = P(seq + DEV_AXES, None)
    return jax.shard_map(
        per_device, mesh=fine, in_specs=in_specs, out_specs=out_specs, check_vma=False
    )
```

```python
import jax
import jax.numpy as jnp
import numpy as np
from jax import lax
from jax.sharding import Mesh
from jax.sharding import PartitionSpec as P

PAIR = 2

highest = lax.Precision.HIGHEST

SEQ_AXES = ("y", "x", "c")
TOK_AXES = ("y", "x")
DEV_AXES = ("e", "p")


def chain_join(earlier, later):
    scale = jnp.exp(later[:, -1:, :])
    state = scale * earlier[:, :-1, :] + later[:, :-1, :]
    return jnp.concatenate([state, earlier[:, -1:, :] + later[:, -1:, :]], axis=1)


def shifted(value, shift, count):
    pairs = [(i, i + shift) for i in range(count - shift)]
    return lax.ppermute(value, SEQ_AXES, pairs)


def carried_in(log_total, local_state, count):
    width = local_state.shape[-1]
    window = jnp.concatenate(
        [local_state, jnp.broadcast_to(log_total[:, None, None], (log_total.shape[0], 1, width))],
        axis=1,
    )
    earlier = None
    shift = 1
    while shift < count:
        arrived = shifted(window, shift, count)
        earlier = arrived if earlier is None else chain_join(arrived, earlier)
        if 2 * shift < count:
            window = chain_join(arrived, window)
        shift *= 2
    return earlier[:, :-1, :]


def head_norm(attention, gain):
    square_mean = jnp.mean(attention * attention, axis=-1, keepdims=True)
    return (attention * lax.rsqrt(square_mean + 1e-06) * gain).astype(jnp.bfloat16)


def slot_ranks(flat_experts, experts):
    onehot = (flat_experts[..., None] == jnp.arange(experts, dtype=jnp.int32)).astype(jnp.int32)
    before = jnp.cumsum(onehot, axis=-2) - onehot
    return jnp.sum(before * onehot, axis=-1)


def per_device(
    queries,
    key_vectors,
    value_vectors,
    log_decay,
    head_gain,
    gate_weight,
    up_weight,
    down_weight,
    expert_ids,
    expert_weights,
):
    count = 1
    for name in SEQ_AXES:
        count *= lax.axis_size(name)
    dev_count = lax.axis_size("e") * lax.axis_size("p")
    experts = dev_count // PAIR

    ids_all = lax.all_gather(expert_ids, DEV_AXES, axis=0, tiled=False)
    partner = [(0, 1), (1, 0)]
    gate_up = jnp.stack([gate_weight[0], up_weight[0]])
    gate_up, ids_all = lax.optimization_barrier((gate_up, ids_all))
    down_core = lax.all_gather(down_weight[0], "c", axis=0, tiled=True)
    gate_up = jnp.concatenate([gate_up, lax.ppermute(gate_up, "p", partner)], axis=2)

    tok_count = expert_ids.shape[0]
    top_count = expert_ids.shape[1]
    capacity = max(2, (3 * tok_count * top_count + 2 * experts - 1) // (2 * experts))
    capacity = -(-capacity // PAIR) * PAIR
    half = capacity // PAIR

    seq_len = queries.shape[0]
    heads = log_decay.shape[1]
    head_dim = queries.shape[1] // heads
    queries_h = jnp.transpose(queries.reshape(seq_len, heads, head_dim), (1, 0, 2))
    keys_h = jnp.transpose(key_vectors.reshape(seq_len, heads, head_dim), (1, 0, 2))
    values_h = jnp.transpose(value_vectors.reshape(seq_len, heads, head_dim), (1, 0, 2))
    decay_h = jnp.transpose(log_decay, (1, 0))
    running = jnp.cumsum(decay_h, axis=1)
    log_total = running[:, -1]
    tail_decay = jnp.exp(log_total[:, None] - running)
    keys_f = keys_h.astype(jnp.float32)
    values_f = values_h.astype(jnp.float32)
    local_state = jnp.einsum(
        "hsa,hsb->hab", keys_f * tail_decay[:, :, None], values_f, precision=highest
    )
    incoming = carried_in(log_total, local_state, count)

    causal = jnp.arange(seq_len)[:, None] >= jnp.arange(seq_len)[None, :]
    spread = jnp.where(causal[None], running[:, :, None] - running[:, None, :], 0.0)
    factors = jnp.where(causal[None], jnp.exp(spread), 0.0)
    scores = (
        jnp.einsum("hta,hsa->hts", queries_h, keys_h, preferred_element_type=jnp.float32) * factors
    )
    carried = jnp.exp(running)[:, :, None] * jnp.einsum(
        "hta,hab->htb", queries_h.astype(jnp.float32), incoming, precision=highest
    )
    attention = jnp.einsum("hts,hsb->htb", scores, values_f, precision=highest) + carried
    normed_h = head_norm(attention, head_gain.reshape(heads, 1, head_dim))
    normed = jnp.transpose(normed_h, (1, 0, 2)).reshape(seq_len, heads * head_dim)

    per_dev = dev_count * half
    flat = ids_all.reshape(dev_count, tok_count * top_count)
    rank = slot_ranks(flat, experts)
    source = jnp.arange(dev_count, dtype=jnp.int32)[:, None]
    slot_index = (flat * PAIR + rank // half) * per_dev + source * half + rank % half
    token_local = source * tok_count + jnp.arange(tok_count * top_count, dtype=jnp.int32)[None, :] // top_count
    slot_token = (
        jnp.full((dev_count * per_dev,), seq_len, jnp.int32)
        .at[slot_index.reshape(-1)]
        .set(token_local.reshape(-1))
    )
    padded = jnp.concatenate([normed, jnp.zeros((1, normed.shape[1]), normed.dtype)], axis=0)
    send_rows = padded[slot_token].reshape(dev_count, per_dev, -1)
    gate_up, send_rows = lax.optimization_barrier((gate_up, send_rows))
    gate_up = lax.all_gather(gate_up, "c", axis=2, tiled=True)
    arrived = lax.all_to_all(send_rows, DEV_AXES, split_axis=0, concat_axis=0, tiled=True)
    down_core, arrived = lax.optimization_barrier((down_core, arrived))
    down_far = lax.ppermute(down_core, "p", partner)
    local_rows = jnp.transpose(arrived, (1, 0, 2)).reshape(per_dev, -1)
    width = local_rows.shape[1]
    groups = 1
    for name in TOK_AXES:
        groups *= lax.axis_size(name)
    piece = lax.all_to_all(
        jnp.broadcast_to(local_rows[None], (groups,) + local_rows.shape),
        TOK_AXES,
        split_axis=0,
        concat_axis=0,
        tiled=True,
    ).reshape(groups * per_dev, width)
    down_far, piece = lax.optimization_barrier((down_far, piece))
    cores = down_far.shape[0] // down_weight.shape[1]
    down_all = jnp.stack(
        [down_core.reshape(cores, -1, width), down_far.reshape(cores, -1, width)], axis=1
    ).reshape(-1, width)
    gate_part = jnp.dot(piece, gate_up[0], preferred_element_type=jnp.float32)
    up_part = jnp.dot(piece, gate_up[1], preferred_element_type=jnp.float32)
    hidden_all = (jax.nn.silu(gate_part) * up_part).astype(jnp.bfloat16)
    term = jnp.dot(hidden_all, down_all, preferred_element_type=jnp.float32).astype(jnp.bfloat16)
    parts = lax.all_to_all(
        term.reshape(groups, per_dev, width), TOK_AXES, split_axis=0, concat_axis=0, tiled=True
    )
    summed = jnp.sum(parts.astype(jnp.float32), axis=0).astype(jnp.bfloat16)
    returned = lax.all_to_all(
        summed.reshape(dev_count, half, width),
        DEV_AXES,
        split_axis=0,
        concat_axis=0,
        tiled=True,
    )
    own = lax.axis_index(DEV_AXES)
    own_flat = lax.dynamic_index_in_dim(flat, own, 0, False)
    own_rank = lax.dynamic_index_in_dim(rank, own, 0, False)
    pick_index = own_flat * capacity + own_rank
    picked = returned.reshape(dev_count * half, width)[pick_index].reshape(
        tok_count, top_count, width
    )
    combined = jnp.sum(picked.astype(jnp.float32) * expert_weights[:, :, None], axis=1)
    return combined.astype(jnp.bfloat16)


def split_mesh(mesh):
    devices = mesh.devices
    seq_count, dev_count = devices.shape
    cores = 2
    xs = 4
    flat = devices.reshape(-1)
    if hasattr(flat[0], "coords"):
        cores = len({int(getattr(d, "core_on_chip", 0)) for d in flat})
        xs = len({int(d.coords[0]) for d in flat})
    ys = seq_count // (xs * cores)
    shape = (ys, xs, cores, dev_count // PAIR, PAIR)
    return Mesh(devices.reshape(shape), ("y", "x", "c", "e", "p"))


def solution(mesh):
    fine = split_mesh(mesh)
    seq = SEQ_AXES
    in_specs = (
        P(seq, DEV_AXES),
        P(seq, DEV_AXES),
        P(seq, DEV_AXES),
        P(seq, DEV_AXES),
        P(DEV_AXES),
        P(DEV_AXES, None, seq),
        P(DEV_AXES, None, seq),
        P(DEV_AXES, seq, None),
        P(seq + DEV_AXES, None),
        P(seq + DEV_AXES, None),
    )
    out_specs = P(seq + DEV_AXES, None)
    return jax.shard_map(
        per_device, mesh=fine, in_specs=in_specs, out_specs=out_specs, check_vma=False
    )
```

```python
import jax
import jax.numpy as jnp
import numpy as np
from jax import lax
from jax.sharding import Mesh
from jax.sharding import PartitionSpec as P

PAIR = 2

highest = lax.Precision.HIGHEST

SEQ_AXES = ("y", "x", "c")
TOK_AXES = ("y", "x")
DEV_AXES = ("e", "p")


def chain_join(earlier, later):
    scale = jnp.exp(later[:, -1:, :])
    state = scale * earlier[:, :-1, :] + later[:, :-1, :]
    return jnp.concatenate([state, earlier[:, -1:, :] + later[:, -1:, :]], axis=1)


def shifted(value, shift, count):
    pairs = [(i, i + shift) for i in range(count - shift)]
    return lax.ppermute(value, SEQ_AXES, pairs)


def carried_in(log_total, local_state, count):
    width = local_state.shape[-1]
    window = jnp.concatenate(
        [local_state, jnp.broadcast_to(log_total[:, None, None], (log_total.shape[0], 1, width))],
        axis=1,
    )
    earlier = None
    shift = 1
    while shift < count:
        arrived = shifted(window, shift, count)
        earlier = arrived if earlier is None else chain_join(arrived, earlier)
        if 2 * shift < count:
            window = chain_join(arrived, window)
        shift *= 2
    return earlier[:, :-1, :]


def head_norm(attention, gain):
    square_mean = jnp.mean(attention * attention, axis=-1, keepdims=True)
    return (attention * lax.rsqrt(square_mean + 1e-06) * gain).astype(jnp.bfloat16)


def slot_ranks(flat_experts, experts):
    onehot = (flat_experts[..., None] == jnp.arange(experts, dtype=jnp.int32)).astype(jnp.int32)
    before = jnp.cumsum(onehot, axis=-2) - onehot
    return jnp.sum(before * onehot, axis=-1)


def per_device(
    queries,
    key_vectors,
    value_vectors,
    log_decay,
    head_gain,
    gate_weight,
    up_weight,
    down_weight,
    expert_ids,
    expert_weights,
):
    count = 1
    for name in SEQ_AXES:
        count *= lax.axis_size(name)
    dev_count = lax.axis_size("e") * lax.axis_size("p")
    experts = dev_count // PAIR

    ids_all = lax.all_gather(expert_ids, DEV_AXES, axis=0, tiled=False)
    partner = [(0, 1), (1, 0)]
    gate_up = jnp.stack([gate_weight[0], up_weight[0]])
    gate_up, ids_all = lax.optimization_barrier((gate_up, ids_all))
    gate_up_core = lax.all_gather(gate_up, "c", axis=2, tiled=True)
    down_core = lax.all_gather(down_weight[0], "c", axis=0, tiled=True)
    gate_up_far = lax.ppermute(gate_up, "p", partner)

    tok_count = expert_ids.shape[0]
    top_count = expert_ids.shape[1]
    capacity = max(2, (3 * tok_count * top_count + 2 * experts - 1) // (2 * experts))
    capacity = -(-capacity // PAIR) * PAIR
    half = capacity // PAIR

    seq_len = queries.shape[0]
    heads = log_decay.shape[1]
    head_dim = queries.shape[1] // heads
    queries_h = jnp.transpose(queries.reshape(seq_len, heads, head_dim), (1, 0, 2))
    keys_h = jnp.transpose(key_vectors.reshape(seq_len, heads, head_dim), (1, 0, 2))
    values_h = jnp.transpose(value_vectors.reshape(seq_len, heads, head_dim), (1, 0, 2))
    decay_h = jnp.transpose(log_decay, (1, 0))
    running = jnp.cumsum(decay_h, axis=1)
    log_total = running[:, -1]
    tail_decay = jnp.exp(log_total[:, None] - running)
    keys_f = keys_h.astype(jnp.float32)
    values_f = values_h.astype(jnp.float32)
    local_state = jnp.einsum(
        "hsa,hsb->hab", keys_f * tail_decay[:, :, None], values_f, precision=highest
    )
    incoming = carried_in(log_total, local_state, count)

    causal = jnp.arange(seq_len)[:, None] >= jnp.arange(seq_len)[None, :]
    spread = jnp.where(causal[None], running[:, :, None] - running[:, None, :], 0.0)
    factors = jnp.where(causal[None], jnp.exp(spread), 0.0)
    scores = (
        jnp.einsum("hta,hsa->hts", queries_h, keys_h, preferred_element_type=jnp.float32) * factors
    )
    carried = jnp.exp(running)[:, :, None] * jnp.einsum(
        "hta,hab->htb", queries_h.astype(jnp.float32), incoming, precision=highest
    )
    attention = jnp.einsum("hts,hsb->htb", scores, values_f, precision=highest) + carried
    normed_h = head_norm(attention, head_gain.reshape(heads, 1, head_dim))
    normed = jnp.transpose(normed_h, (1, 0, 2)).reshape(seq_len, heads * head_dim)

    per_dev = dev_count * half
    flat = ids_all.reshape(dev_count, tok_count * top_count)
    rank = slot_ranks(flat, experts)
    source = jnp.arange(dev_count, dtype=jnp.int32)[:, None]
    slot_index = (flat * PAIR + rank // half) * per_dev + source * half + rank % half
    token_local = source * tok_count + jnp.arange(tok_count * top_count, dtype=jnp.int32)[None, :] // top_count
    slot_token = (
        jnp.full((dev_count * per_dev,), seq_len, jnp.int32)
        .at[slot_index.reshape(-1)]
        .set(token_local.reshape(-1))
    )
    padded = jnp.concatenate([normed, jnp.zeros((1, normed.shape[1]), normed.dtype)], axis=0)
    send_rows = padded[slot_token].reshape(dev_count, per_dev, -1)
    gate_up_far, send_rows = lax.optimization_barrier((gate_up_far, send_rows))
    gate_up_far = lax.all_gather(gate_up_far, "c", axis=2, tiled=True)
    arrived = lax.all_to_all(send_rows, DEV_AXES, split_axis=0, concat_axis=0, tiled=True)
    down_core, arrived = lax.optimization_barrier((down_core, arrived))
    down_far = lax.ppermute(down_core, "p", partner)
    local_rows = jnp.transpose(arrived, (1, 0, 2)).reshape(per_dev, -1)
    width = local_rows.shape[1]
    groups = 1
    for name in TOK_AXES:
        groups *= lax.axis_size(name)
    piece = lax.all_to_all(
        jnp.broadcast_to(local_rows[None], (groups,) + local_rows.shape),
        TOK_AXES,
        split_axis=0,
        concat_axis=0,
        tiled=True,
    ).reshape(groups * per_dev, width)
    down_far, piece = lax.optimization_barrier((down_far, piece))

    def hidden_of(weights):
        gate_part = jnp.dot(piece, weights[0], preferred_element_type=jnp.float32)
        up_part = jnp.dot(piece, weights[1], preferred_element_type=jnp.float32)
        return (jax.nn.silu(gate_part) * up_part).astype(jnp.bfloat16)

    term = (
        jnp.dot(hidden_of(gate_up_core), down_core, preferred_element_type=jnp.float32)
        + jnp.dot(hidden_of(gate_up_far), down_far, preferred_element_type=jnp.float32)
    ).astype(jnp.bfloat16)
    parts = lax.all_to_all(
        term.reshape(groups, per_dev, width), TOK_AXES, split_axis=0, concat_axis=0, tiled=True
    )
    summed = jnp.sum(parts.astype(jnp.float32), axis=0).astype(jnp.bfloat16)
    returned = lax.all_to_all(
        summed.reshape(dev_count, half, width),
        DEV_AXES,
        split_axis=0,
        concat_axis=0,
        tiled=True,
    )
    own = lax.axis_index(DEV_AXES)
    own_flat = lax.dynamic_index_in_dim(flat, own, 0, False)
    own_rank = lax.dynamic_index_in_dim(rank, own, 0, False)
    pick_index = own_flat * capacity + own_rank
    picked = returned.reshape(dev_count * half, width)[pick_index].reshape(
        tok_count, top_count, width
    )
    combined = jnp.sum(picked.astype(jnp.float32) * expert_weights[:, :, None], axis=1)
    return combined.astype(jnp.bfloat16)


def split_mesh(mesh):
    devices = mesh.devices
    seq_count, dev_count = devices.shape
    cores = 2
    xs = 4
    flat = devices.reshape(-1)
    if hasattr(flat[0], "coords"):
        cores = len({int(getattr(d, "core_on_chip", 0)) for d in flat})
        xs = len({int(d.coords[0]) for d in flat})
    ys = seq_count // (xs * cores)
    shape = (ys, xs, cores, dev_count // PAIR, PAIR)
    return Mesh(devices.reshape(shape), ("y", "x", "c", "e", "p"))


def solution(mesh):
    fine = split_mesh(mesh)
    seq = SEQ_AXES
    in_specs = (
        P(seq, DEV_AXES),
        P(seq, DEV_AXES),
        P(seq, DEV_AXES),
        P(seq, DEV_AXES),
        P(DEV_AXES),
        P(DEV_AXES, None, seq),
        P(DEV_AXES, None, seq),
        P(DEV_AXES, seq, None),
        P(seq + DEV_AXES, None),
        P(seq + DEV_AXES, None),
    )
    out_specs = P(seq + DEV_AXES, None)
    return jax.shard_map(
        per_device, mesh=fine, in_specs=in_specs, out_specs=out_specs, check_vma=False
    )
```

```python
import jax
import jax.numpy as jnp
import numpy as np
from jax import lax
from jax.sharding import Mesh
from jax.sharding import PartitionSpec as P

PAIR = 2

highest = lax.Precision.HIGHEST

SEQ_AXES = ("y", "x", "c")
TOK_AXES = ("y", "x")
DEV_AXES = ("e", "p")


def chain_join(earlier, later):
    scale = jnp.exp(later[:, -1:, :])
    state = scale * earlier[:, :-1, :] + later[:, :-1, :]
    return jnp.concatenate([state, earlier[:, -1:, :] + later[:, -1:, :]], axis=1)


def shifted(value, shift, count):
    pairs = [(i, i + shift) for i in range(count - shift)]
    return lax.ppermute(value, SEQ_AXES, pairs)


def carried_in(log_total, local_state, count):
    width = local_state.shape[-1]
    window = jnp.concatenate(
        [local_state, jnp.broadcast_to(log_total[:, None, None], (log_total.shape[0], 1, width))],
        axis=1,
    )
    earlier = None
    shift = 1
    while shift < count:
        arrived = shifted(window, shift, count)
        earlier = arrived if earlier is None else chain_join(arrived, earlier)
        if 2 * shift < count:
            window = chain_join(arrived, window)
        shift *= 2
    return earlier[:, :-1, :]


def head_norm(attention, gain):
    square_mean = jnp.mean(attention * attention, axis=-1, keepdims=True)
    return (attention * lax.rsqrt(square_mean + 1e-06) * gain).astype(jnp.bfloat16)


def slot_ranks(flat_experts, experts):
    onehot = (flat_experts[..., None] == jnp.arange(experts, dtype=jnp.int32)).astype(jnp.int32)
    before = jnp.cumsum(onehot, axis=-2) - onehot
    return jnp.sum(before * onehot, axis=-1)


def per_device(
    queries,
    key_vectors,
    value_vectors,
    log_decay,
    head_gain,
    gate_weight,
    up_weight,
    down_weight,
    expert_ids,
    expert_weights,
):
    count = 1
    for name in SEQ_AXES:
        count *= lax.axis_size(name)
    dev_count = lax.axis_size("e") * lax.axis_size("p")
    experts = dev_count // PAIR

    ids_all = lax.all_gather(expert_ids, DEV_AXES, axis=0, tiled=False)
    partner = [(0, 1), (1, 0)]
    gate_up = jnp.stack([gate_weight[0], up_weight[0]])
    gate_up, ids_all = lax.optimization_barrier((gate_up, ids_all))
    gate_up_core = lax.all_gather(gate_up, "c", axis=2, tiled=True)
    down_core = lax.all_gather(down_weight[0], "c", axis=0, tiled=True)
    gate_up_far = lax.ppermute(gate_up, "p", partner)

    tok_count = expert_ids.shape[0]
    top_count = expert_ids.shape[1]
    capacity = max(2, (3 * tok_count * top_count + 2 * experts - 1) // (2 * experts))
    capacity = -(-capacity // PAIR) * PAIR
    half = capacity // PAIR

    seq_len = queries.shape[0]
    heads = log_decay.shape[1]
    head_dim = queries.shape[1] // heads
    queries_h = jnp.transpose(queries.reshape(seq_len, heads, head_dim), (1, 0, 2))
    keys_h = jnp.transpose(key_vectors.reshape(seq_len, heads, head_dim), (1, 0, 2))
    values_h = jnp.transpose(value_vectors.reshape(seq_len, heads, head_dim), (1, 0, 2))
    decay_h = jnp.transpose(log_decay, (1, 0))
    running = jnp.cumsum(decay_h, axis=1)
    log_total = running[:, -1]
    tail_decay = jnp.exp(log_total[:, None] - running)
    keys_f = keys_h.astype(jnp.float32)
    values_f = values_h.astype(jnp.float32)
    local_state = jnp.einsum(
        "hsa,hsb->hab", keys_f * tail_decay[:, :, None], values_f, precision=highest
    )
    incoming = carried_in(log_total, local_state, count)

    causal = jnp.arange(seq_len)[:, None] >= jnp.arange(seq_len)[None, :]
    spread = jnp.where(causal[None], running[:, :, None] - running[:, None, :], 0.0)
    factors = jnp.where(causal[None], jnp.exp(spread), 0.0)
    scores = (
        jnp.einsum("hta,hsa->hts", queries_h, keys_h, preferred_element_type=jnp.float32) * factors
    )
    carried = jnp.exp(running)[:, :, None] * jnp.einsum(
        "hta,hab->htb", queries_h.astype(jnp.float32), incoming, precision=highest
    )
    attention = jnp.einsum("hts,hsb->htb", scores, values_f, precision=highest) + carried
    normed_h = head_norm(attention, head_gain.reshape(heads, 1, head_dim))
    normed = jnp.transpose(normed_h, (1, 0, 2)).reshape(seq_len, heads * head_dim)

    per_dev = dev_count * half
    flat = ids_all.reshape(dev_count, tok_count * top_count)
    rank = slot_ranks(flat, experts)
    source = jnp.arange(dev_count, dtype=jnp.int32)[:, None]
    slot_index = (flat * PAIR + rank // half) * per_dev + source * half + rank % half
    token_local = source * tok_count + jnp.arange(tok_count * top_count, dtype=jnp.int32)[None, :] // top_count
    slot_token = (
        jnp.full((dev_count * per_dev,), seq_len, jnp.int32)
        .at[slot_index.reshape(-1)]
        .set(token_local.reshape(-1))
    )
    padded = jnp.concatenate([normed, jnp.zeros((1, normed.shape[1]), normed.dtype)], axis=0)
    send_rows = padded[slot_token].reshape(dev_count, per_dev, -1)
    gate_up_far, send_rows = lax.optimization_barrier((gate_up_far, send_rows))
    gate_up_far = lax.all_gather(gate_up_far, "c", axis=2, tiled=True)
    arrived = lax.all_to_all(send_rows, DEV_AXES, split_axis=0, concat_axis=0, tiled=True)
    down_core, arrived = lax.optimization_barrier((down_core, arrived))
    down_far = lax.ppermute(down_core, "p", partner)
    local_rows = jnp.transpose(arrived, (1, 0, 2)).reshape(per_dev, -1)
    width = local_rows.shape[1]
    groups = 1
    for name in TOK_AXES:
        groups *= lax.axis_size(name)
    piece = lax.all_to_all(
        jnp.broadcast_to(local_rows[None], (groups,) + local_rows.shape),
        TOK_AXES,
        split_axis=0,
        concat_axis=0,
        tiled=True,
    ).reshape(groups * per_dev, width)
    down_far, piece = lax.optimization_barrier((down_far, piece))

    def hidden_of(weights):
        gate_part = jnp.dot(piece, weights[0], preferred_element_type=jnp.float32)
        up_part = jnp.dot(piece, weights[1], preferred_element_type=jnp.float32)
        return (jax.nn.silu(gate_part) * up_part).astype(jnp.bfloat16)

    hidden_all = jnp.concatenate([hidden_of(gate_up_core), hidden_of(gate_up_far)], axis=1)
    down_all = jnp.concatenate([down_core, down_far], axis=0)
    term = jnp.dot(hidden_all, down_all, preferred_element_type=jnp.float32).astype(jnp.bfloat16)
    parts = lax.all_to_all(
        term.reshape(groups, per_dev, width), TOK_AXES, split_axis=0, concat_axis=0, tiled=True
    )
    summed = jnp.sum(parts.astype(jnp.float32), axis=0).astype(jnp.bfloat16)
    returned = lax.all_to_all(
        summed.reshape(dev_count, half, width),
        DEV_AXES,
        split_axis=0,
        concat_axis=0,
        tiled=True,
    )
    own = lax.axis_index(DEV_AXES)
    own_flat = lax.dynamic_index_in_dim(flat, own, 0, False)
    own_rank = lax.dynamic_index_in_dim(rank, own, 0, False)
    pick_index = own_flat * capacity + own_rank
    picked = returned.reshape(dev_count * half, width)[pick_index].reshape(
        tok_count, top_count, width
    )
    combined = jnp.sum(picked.astype(jnp.float32) * expert_weights[:, :, None], axis=1)
    return combined.astype(jnp.bfloat16)


def split_mesh(mesh):
    devices = mesh.devices
    seq_count, dev_count = devices.shape
    cores = 2
    xs = 4
    flat = devices.reshape(-1)
    if hasattr(flat[0], "coords"):
        cores = len({int(getattr(d, "core_on_chip", 0)) for d in flat})
        xs = len({int(d.coords[0]) for d in flat})
    ys = seq_count // (xs * cores)
    shape = (ys, xs, cores, dev_count // PAIR, PAIR)
    return Mesh(devices.reshape(shape), ("y", "x", "c", "e", "p"))


def solution(mesh):
    fine = split_mesh(mesh)
    seq = SEQ_AXES
    in_specs = (
        P(seq, DEV_AXES),
        P(seq, DEV_AXES),
        P(seq, DEV_AXES),
        P(seq, DEV_AXES),
        P(DEV_AXES),
        P(DEV_AXES, None, seq),
        P(DEV_AXES, None, seq),
        P(DEV_AXES, seq, None),
        P(seq + DEV_AXES, None),
        P(seq + DEV_AXES, None),
    )
    out_specs = P(seq + DEV_AXES, None)
    return jax.shard_map(
        per_device, mesh=fine, in_specs=in_specs, out_specs=out_specs, check_vma=False
    )
```

```python
import jax
import jax.numpy as jnp
import numpy as np
from jax import lax
from jax.sharding import Mesh
from jax.sharding import PartitionSpec as P

PAIR = 2

highest = lax.Precision.HIGHEST

SEQ_AXES = ("y", "x", "c")
TOK_AXES = ("y", "x")
DEV_AXES = ("e", "p")


def chain_join(earlier, later):
    scale = jnp.exp(later[:, -1:, :])
    state = scale * earlier[:, :-1, :] + later[:, :-1, :]
    return jnp.concatenate([state, earlier[:, -1:, :] + later[:, -1:, :]], axis=1)


def shifted(value, shift, count):
    pairs = [(i, i + shift) for i in range(count - shift)]
    return lax.ppermute(value.astype(jnp.bfloat16), SEQ_AXES, pairs).astype(value.dtype)


def carried_in(log_total, local_state, count):
    width = local_state.shape[-1]
    window = jnp.concatenate(
        [local_state, jnp.broadcast_to(log_total[:, None, None], (log_total.shape[0], 1, width))],
        axis=1,
    )
    earlier = None
    shift = 1
    while shift < count:
        arrived = shifted(window, shift, count)
        earlier = arrived if earlier is None else chain_join(arrived, earlier)
        if 2 * shift < count:
            window = chain_join(arrived, window)
        shift *= 2
    return earlier[:, :-1, :]


def head_norm(attention, gain):
    square_mean = jnp.mean(attention * attention, axis=-1, keepdims=True)
    return (attention * lax.rsqrt(square_mean + 1e-06) * gain).astype(jnp.bfloat16)


def slot_ranks(flat_experts, experts):
    onehot = (flat_experts[..., None] == jnp.arange(experts, dtype=jnp.int32)).astype(jnp.int32)
    before = jnp.cumsum(onehot, axis=-2) - onehot
    return jnp.sum(before * onehot, axis=-1)


def per_device(
    queries,
    key_vectors,
    value_vectors,
    log_decay,
    head_gain,
    gate_weight,
    up_weight,
    down_weight,
    expert_ids,
    expert_weights,
):
    count = 1
    for name in SEQ_AXES:
        count *= lax.axis_size(name)
    dev_count = lax.axis_size("e") * lax.axis_size("p")
    experts = dev_count // PAIR

    ids_all = lax.all_gather(expert_ids, DEV_AXES, axis=0, tiled=False)
    partner = [(0, 1), (1, 0)]
    gate_up = jnp.stack([gate_weight[0], up_weight[0]])
    gate_up, ids_all = lax.optimization_barrier((gate_up, ids_all))
    gate_up_core = lax.all_gather(gate_up, "c", axis=2, tiled=True)
    down_core = lax.all_gather(down_weight[0], "c", axis=0, tiled=True)
    gate_up_far = lax.ppermute(gate_up, "p", partner)

    tok_count = expert_ids.shape[0]
    top_count = expert_ids.shape[1]
    capacity = max(2, (3 * tok_count * top_count + 2 * experts - 1) // (2 * experts))
    capacity = -(-capacity // PAIR) * PAIR
    half = capacity // PAIR

    seq_len = queries.shape[0]
    heads = log_decay.shape[1]
    head_dim = queries.shape[1] // heads
    queries_h = jnp.transpose(queries.reshape(seq_len, heads, head_dim), (1, 0, 2))
    keys_h = jnp.transpose(key_vectors.reshape(seq_len, heads, head_dim), (1, 0, 2))
    values_h = jnp.transpose(value_vectors.reshape(seq_len, heads, head_dim), (1, 0, 2))
    decay_h = jnp.transpose(log_decay, (1, 0))
    running = jnp.cumsum(decay_h, axis=1)
    log_total = running[:, -1]
    tail_decay = jnp.exp(log_total[:, None] - running)
    keys_f = keys_h.astype(jnp.float32)
    values_f = values_h.astype(jnp.float32)
    local_state = jnp.einsum(
        "hsa,hsb->hab", keys_f * tail_decay[:, :, None], values_f, precision=highest
    )
    incoming = carried_in(log_total, local_state, count)

    causal = jnp.arange(seq_len)[:, None] >= jnp.arange(seq_len)[None, :]
    spread = jnp.where(causal[None], running[:, :, None] - running[:, None, :], 0.0)
    factors = jnp.where(causal[None], jnp.exp(spread), 0.0)
    scores = (
        jnp.einsum("hta,hsa->hts", queries_h, keys_h, preferred_element_type=jnp.float32) * factors
    )
    carried = jnp.exp(running)[:, :, None] * jnp.einsum(
        "hta,hab->htb", queries_h.astype(jnp.float32), incoming, precision=highest
    )
    attention = jnp.einsum("hts,hsb->htb", scores, values_f, precision=highest) + carried
    normed_h = head_norm(attention, head_gain.reshape(heads, 1, head_dim))
    normed = jnp.transpose(normed_h, (1, 0, 2)).reshape(seq_len, heads * head_dim)

    per_dev = dev_count * half
    flat = ids_all.reshape(dev_count, tok_count * top_count)
    rank = slot_ranks(flat, experts)
    source = jnp.arange(dev_count, dtype=jnp.int32)[:, None]
    slot_index = (flat * PAIR + rank // half) * per_dev + source * half + rank % half
    token_local = source * tok_count + jnp.arange(tok_count * top_count, dtype=jnp.int32)[None, :] // top_count
    slot_token = (
        jnp.full((dev_count * per_dev,), seq_len, jnp.int32)
        .at[slot_index.reshape(-1)]
        .set(token_local.reshape(-1))
    )
    padded = jnp.concatenate([normed, jnp.zeros((1, normed.shape[1]), normed.dtype)], axis=0)
    send_rows = padded[slot_token].reshape(dev_count, per_dev, -1)
    gate_up_far, send_rows = lax.optimization_barrier((gate_up_far, send_rows))
    gate_up_far = lax.all_gather(gate_up_far, "c", axis=2, tiled=True)
    arrived = lax.all_to_all(send_rows, DEV_AXES, split_axis=0, concat_axis=0, tiled=True)
    down_core, arrived = lax.optimization_barrier((down_core, arrived))
    down_far = lax.ppermute(down_core, "p", partner)
    local_rows = jnp.transpose(arrived, (1, 0, 2)).reshape(per_dev, -1)
    width = local_rows.shape[1]
    groups = 1
    for name in TOK_AXES:
        groups *= lax.axis_size(name)
    piece = lax.all_to_all(
        jnp.broadcast_to(local_rows[None], (groups,) + local_rows.shape),
        TOK_AXES,
        split_axis=0,
        concat_axis=0,
        tiled=True,
    ).reshape(groups * per_dev, width)
    down_far, piece = lax.optimization_barrier((down_far, piece))

    def hidden_of(weights):
        gate_part = jnp.dot(piece, weights[0], preferred_element_type=jnp.float32)
        up_part = jnp.dot(piece, weights[1], preferred_element_type=jnp.float32)
        return (jax.nn.silu(gate_part) * up_part).astype(jnp.bfloat16)

    hidden_all = jnp.concatenate([hidden_of(gate_up_core), hidden_of(gate_up_far)], axis=1)
    down_all = jnp.concatenate([down_core, down_far], axis=0)
    term = jnp.dot(hidden_all, down_all, preferred_element_type=jnp.float32).astype(jnp.bfloat16)
    parts = lax.all_to_all(
        term.reshape(groups, per_dev, width), TOK_AXES, split_axis=0, concat_axis=0, tiled=True
    )
    summed = jnp.sum(parts.astype(jnp.float32), axis=0).astype(jnp.bfloat16)
    returned = lax.all_to_all(
        summed.reshape(dev_count, half, width),
        DEV_AXES,
        split_axis=0,
        concat_axis=0,
        tiled=True,
    )
    own = lax.axis_index(DEV_AXES)
    own_flat = lax.dynamic_index_in_dim(flat, own, 0, False)
    own_rank = lax.dynamic_index_in_dim(rank, own, 0, False)
    pick_index = own_flat * capacity + own_rank
    picked = returned.reshape(dev_count * half, width)[pick_index].reshape(
        tok_count, top_count, width
    )
    combined = jnp.sum(picked.astype(jnp.float32) * expert_weights[:, :, None], axis=1)
    return combined.astype(jnp.bfloat16)


def split_mesh(mesh):
    devices = mesh.devices
    seq_count, dev_count = devices.shape
    cores = 2
    xs = 4
    flat = devices.reshape(-1)
    if hasattr(flat[0], "coords"):
        cores = len({int(getattr(d, "core_on_chip", 0)) for d in flat})
        xs = len({int(d.coords[0]) for d in flat})
    ys = seq_count // (xs * cores)
    shape = (ys, xs, cores, dev_count // PAIR, PAIR)
    return Mesh(devices.reshape(shape), ("y", "x", "c", "e", "p"))


def solution(mesh):
    fine = split_mesh(mesh)
    seq = SEQ_AXES
    in_specs = (
        P(seq, DEV_AXES),
        P(seq, DEV_AXES),
        P(seq, DEV_AXES),
        P(seq, DEV_AXES),
        P(DEV_AXES),
        P(DEV_AXES, None, seq),
        P(DEV_AXES, None, seq),
        P(DEV_AXES, seq, None),
        P(seq + DEV_AXES, None),
        P(seq + DEV_AXES, None),
    )
    out_specs = P(seq + DEV_AXES, None)
    return jax.shard_map(
        per_device, mesh=fine, in_specs=in_specs, out_specs=out_specs, check_vma=False
    )
```

```python
import jax
import jax.numpy as jnp
import numpy as np
from jax import lax
from jax.sharding import Mesh
from jax.sharding import PartitionSpec as P

PAIR = 2

highest = lax.Precision.HIGHEST

SEQ_AXES = ("y", "x", "c")
TOK_AXES = ("y", "x")
DEV_AXES = ("e", "p")


def chain_join(earlier, later):
    scale = jnp.exp(later[:, -1:, :])
    state = scale * earlier[:, :-1, :] + later[:, :-1, :]
    return jnp.concatenate([state, earlier[:, -1:, :] + later[:, -1:, :]], axis=1)


def shifted(value, shift, count):
    pairs = [(i, i + shift) for i in range(count - shift)]
    return lax.ppermute(value.astype(jnp.bfloat16), SEQ_AXES, pairs).astype(value.dtype)


def carried_in(log_total, local_state, count):
    width = local_state.shape[-1]
    window = jnp.concatenate(
        [local_state, jnp.broadcast_to(log_total[:, None, None], (log_total.shape[0], 1, width))],
        axis=1,
    )
    earlier = None
    shift = 1
    while shift < count:
        arrived = shifted(window, shift, count)
        earlier = arrived if earlier is None else chain_join(arrived, earlier)
        if 2 * shift < count:
            window = chain_join(arrived, window)
        shift *= 2
    return earlier[:, :-1, :]


def head_norm(attention, gain):
    square_mean = jnp.mean(attention * attention, axis=-1, keepdims=True)
    return (attention * lax.rsqrt(square_mean + 1e-06) * gain).astype(jnp.bfloat16)


def slot_ranks(flat_experts, experts):
    onehot = (flat_experts[..., None] == jnp.arange(experts, dtype=jnp.int32)).astype(jnp.int32)
    before = jnp.cumsum(onehot, axis=-2) - onehot
    return jnp.sum(before * onehot, axis=-1)


def per_device(
    queries,
    key_vectors,
    value_vectors,
    log_decay,
    head_gain,
    gate_weight,
    up_weight,
    down_weight,
    expert_ids,
    expert_weights,
):
    count = 1
    for name in SEQ_AXES:
        count *= lax.axis_size(name)
    dev_count = lax.axis_size("e") * lax.axis_size("p")
    experts = dev_count // PAIR

    ids_all = lax.all_gather(expert_ids, DEV_AXES, axis=0, tiled=False)
    partner = [(0, 1), (1, 0)]
    gate_up = jnp.stack([gate_weight[0], up_weight[0]])
    gate_up, ids_all = lax.optimization_barrier((gate_up, ids_all))
    gate_up_core = lax.all_gather(gate_up, "c", axis=2, tiled=True)
    down_core = lax.all_gather(down_weight[0], "c", axis=0, tiled=True)
    gate_up_far = lax.ppermute(gate_up, "p", partner)

    tok_count = expert_ids.shape[0]
    top_count = expert_ids.shape[1]
    capacity = max(2, (3 * tok_count * top_count + 2 * experts - 1) // (2 * experts))
    capacity = -(-capacity // PAIR) * PAIR
    half = capacity // PAIR

    seq_len = queries.shape[0]
    heads = log_decay.shape[1]
    head_dim = queries.shape[1] // heads
    queries_h = jnp.transpose(queries.reshape(seq_len, heads, head_dim), (1, 0, 2))
    keys_h = jnp.transpose(key_vectors.reshape(seq_len, heads, head_dim), (1, 0, 2))
    values_h = jnp.transpose(value_vectors.reshape(seq_len, heads, head_dim), (1, 0, 2))
    decay_h = jnp.transpose(log_decay, (1, 0))
    running = jnp.cumsum(decay_h, axis=1)
    log_total = running[:, -1]
    tail_decay = jnp.exp(log_total[:, None] - running)
    keys_f = keys_h.astype(jnp.float32)
    values_f = values_h.astype(jnp.float32)
    local_state = jnp.einsum(
        "hsa,hsb->hab", keys_f * tail_decay[:, :, None], values_f, precision=highest
    )
    incoming = carried_in(log_total, local_state, count)

    causal = jnp.arange(seq_len)[:, None] >= jnp.arange(seq_len)[None, :]
    spread = jnp.where(causal[None], running[:, :, None] - running[:, None, :], 0.0)
    factors = jnp.where(causal[None], jnp.exp(spread), 0.0)
    scores = (
        jnp.einsum("hta,hsa->hts", queries_h, keys_h, preferred_element_type=jnp.float32) * factors
    )
    carried = jnp.exp(running)[:, :, None] * jnp.einsum(
        "hta,hab->htb", queries_h.astype(jnp.float32), incoming, precision=highest
    )
    attention = jnp.einsum("hts,hsb->htb", scores, values_f, precision=highest) + carried
    normed_h = head_norm(attention, head_gain.reshape(heads, 1, head_dim))
    normed = jnp.transpose(normed_h, (1, 0, 2)).reshape(seq_len, heads * head_dim)

    per_dev = dev_count * half
    flat = ids_all.reshape(dev_count, tok_count * top_count)
    rank = slot_ranks(flat, experts)
    source = jnp.arange(dev_count, dtype=jnp.int32)[:, None]
    slot_index = (flat * PAIR + rank // half) * per_dev + source * half + rank % half
    token_local = source * tok_count + jnp.arange(tok_count * top_count, dtype=jnp.int32)[None, :] // top_count
    slot_token = (
        jnp.full((dev_count * per_dev,), seq_len, jnp.int32)
        .at[slot_index.reshape(-1)]
        .set(token_local.reshape(-1))
    )
    padded = jnp.concatenate([normed, jnp.zeros((1, normed.shape[1]), normed.dtype)], axis=0)
    send_rows = padded[slot_token].reshape(dev_count, per_dev, -1)
    gate_up_far, send_rows = lax.optimization_barrier((gate_up_far, send_rows))
    gate_up_far = lax.all_gather(gate_up_far, "c", axis=2, tiled=True)
    arrived = lax.all_to_all(send_rows, DEV_AXES, split_axis=0, concat_axis=0, tiled=True)
    down_core, arrived = lax.optimization_barrier((down_core, arrived))
    down_far = lax.ppermute(down_core, "p", partner)
    local_rows = jnp.transpose(arrived, (1, 0, 2)).reshape(per_dev, -1)
    width = local_rows.shape[1]
    groups = 1
    for name in TOK_AXES:
        groups *= lax.axis_size(name)
    piece = lax.all_to_all(
        jnp.broadcast_to(local_rows[None], (groups,) + local_rows.shape),
        TOK_AXES,
        split_axis=0,
        concat_axis=0,
        tiled=True,
    ).reshape(groups * per_dev, width)
    down_far, piece = lax.optimization_barrier((down_far, piece))

    down_all = jnp.concatenate([down_core, down_far], axis=0)
    rows = piece.reshape(groups, per_dev, width)
    cut = per_dev // 2

    def summed_of(chunk):
        flat_rows = chunk.reshape(-1, width)

        def hidden_of(weights):
            gate_part = jnp.dot(flat_rows, weights[0], preferred_element_type=jnp.float32)
            up_part = jnp.dot(flat_rows, weights[1], preferred_element_type=jnp.float32)
            return (jax.nn.silu(gate_part) * up_part).astype(jnp.bfloat16)

        hidden_all = jnp.concatenate([hidden_of(gate_up_core), hidden_of(gate_up_far)], axis=1)
        term = jnp.dot(hidden_all, down_all, preferred_element_type=jnp.float32).astype(jnp.bfloat16)
        parts = lax.all_to_all(
            term.reshape(chunk.shape), TOK_AXES, split_axis=0, concat_axis=0, tiled=True
        )
        return jnp.sum(parts.astype(jnp.float32), axis=0).astype(jnp.bfloat16)

    summed = jnp.concatenate([summed_of(rows[:, :cut]), summed_of(rows[:, cut:])], axis=0)
    returned = lax.all_to_all(
        summed.reshape(dev_count, half, width),
        DEV_AXES,
        split_axis=0,
        concat_axis=0,
        tiled=True,
    )
    own = lax.axis_index(DEV_AXES)
    own_flat = lax.dynamic_index_in_dim(flat, own, 0, False)
    own_rank = lax.dynamic_index_in_dim(rank, own, 0, False)
    pick_index = own_flat * capacity + own_rank
    picked = returned.reshape(dev_count * half, width)[pick_index].reshape(
        tok_count, top_count, width
    )
    combined = jnp.sum(picked.astype(jnp.float32) * expert_weights[:, :, None], axis=1)
    return combined.astype(jnp.bfloat16)


def split_mesh(mesh):
    devices = mesh.devices
    seq_count, dev_count = devices.shape
    cores = 2
    xs = 4
    flat = devices.reshape(-1)
    if hasattr(flat[0], "coords"):
        cores = len({int(getattr(d, "core_on_chip", 0)) for d in flat})
        xs = len({int(d.coords[0]) for d in flat})
    ys = seq_count // (xs * cores)
    shape = (ys, xs, cores, dev_count // PAIR, PAIR)
    return Mesh(devices.reshape(shape), ("y", "x", "c", "e", "p"))


def solution(mesh):
    fine = split_mesh(mesh)
    seq = SEQ_AXES
    in_specs = (
        P(seq, DEV_AXES),
        P(seq, DEV_AXES),
        P(seq, DEV_AXES),
        P(seq, DEV_AXES),
        P(DEV_AXES),
        P(DEV_AXES, None, seq),
        P(DEV_AXES, None, seq),
        P(DEV_AXES, seq, None),
        P(seq + DEV_AXES, None),
        P(seq + DEV_AXES, None),
    )
    out_specs = P(seq + DEV_AXES, None)
    return jax.shard_map(
        per_device, mesh=fine, in_specs=in_specs, out_specs=out_specs, check_vma=False
    )
```

```python
import jax
import jax.numpy as jnp
import numpy as np
from jax import lax
from jax.sharding import Mesh
from jax.sharding import PartitionSpec as P

PAIR = 2

highest = lax.Precision.HIGHEST

SEQ_AXES = ("y", "x", "c")
TOK_AXES = ("y", "x")
DEV_AXES = ("e", "p")


def chain_join(earlier, later):
    scale = jnp.exp(later[:, -1:, :])
    state = scale * earlier[:, :-1, :] + later[:, :-1, :]
    return jnp.concatenate([state, earlier[:, -1:, :] + later[:, -1:, :]], axis=1)


def shifted(value, shift, count):
    pairs = [(i, i + shift) for i in range(count - shift)]
    return lax.ppermute(value.astype(jnp.bfloat16), SEQ_AXES, pairs).astype(value.dtype)


def carried_in(log_total, local_state, count):
    width = local_state.shape[-1]
    window = jnp.concatenate(
        [local_state, jnp.broadcast_to(log_total[:, None, None], (log_total.shape[0], 1, width))],
        axis=1,
    )
    earlier = None
    shift = 1
    while shift < count:
        arrived = shifted(window, shift, count)
        earlier = arrived if earlier is None else chain_join(arrived, earlier)
        if 2 * shift < count:
            window = chain_join(arrived, window)
        shift *= 2
    return earlier[:, :-1, :]


def head_norm(attention, gain):
    square_mean = jnp.mean(attention * attention, axis=-1, keepdims=True)
    return (attention * lax.rsqrt(square_mean + 1e-06) * gain).astype(jnp.bfloat16)


def slot_ranks(flat_experts, experts):
    onehot = (flat_experts[..., None] == jnp.arange(experts, dtype=jnp.int32)).astype(jnp.int32)
    before = jnp.cumsum(onehot, axis=-2) - onehot
    return jnp.sum(before * onehot, axis=-1)


def per_device(
    queries,
    key_vectors,
    value_vectors,
    log_decay,
    head_gain,
    gate_weight,
    up_weight,
    down_weight,
    expert_ids,
    expert_weights,
):
    count = 1
    for name in SEQ_AXES:
        count *= lax.axis_size(name)
    dev_count = lax.axis_size("e") * lax.axis_size("p")
    experts = dev_count // PAIR

    ids_all = lax.all_gather(expert_ids, DEV_AXES, axis=0, tiled=False)
    partner = [(0, 1), (1, 0)]
    gate_up = jnp.stack([gate_weight[0], up_weight[0]])
    gate_up, ids_all = lax.optimization_barrier((gate_up, ids_all))
    gate_up_core = lax.all_gather(gate_up, "c", axis=2, tiled=True)
    down_core = lax.all_gather(down_weight[0], "c", axis=0, tiled=True)
    gate_up_far = lax.ppermute(gate_up, "p", partner)

    tok_count = expert_ids.shape[0]
    top_count = expert_ids.shape[1]
    capacity = max(2, (3 * tok_count * top_count + 2 * experts - 1) // (2 * experts))
    capacity = -(-capacity // PAIR) * PAIR
    half = capacity // PAIR

    seq_len = queries.shape[0]
    heads = log_decay.shape[1]
    head_dim = queries.shape[1] // heads
    queries_h = jnp.transpose(queries.reshape(seq_len, heads, head_dim), (1, 0, 2))
    keys_h = jnp.transpose(key_vectors.reshape(seq_len, heads, head_dim), (1, 0, 2))
    values_h = jnp.transpose(value_vectors.reshape(seq_len, heads, head_dim), (1, 0, 2))
    decay_h = jnp.transpose(log_decay, (1, 0))
    running = jnp.cumsum(decay_h, axis=1)
    log_total = running[:, -1]
    tail_decay = jnp.exp(log_total[:, None] - running)
    keys_f = keys_h.astype(jnp.float32)
    values_f = values_h.astype(jnp.float32)
    local_state = jnp.einsum(
        "hsa,hsb->hab", keys_f * tail_decay[:, :, None], values_f, precision=highest
    )
    incoming = carried_in(log_total, local_state, count)

    causal = jnp.arange(seq_len)[:, None] >= jnp.arange(seq_len)[None, :]
    spread = jnp.where(causal[None], running[:, :, None] - running[:, None, :], 0.0)
    factors = jnp.where(causal[None], jnp.exp(spread), 0.0)
    scores = (
        jnp.einsum("hta,hsa->hts", queries_h, keys_h, preferred_element_type=jnp.float32) * factors
    )
    carried = jnp.exp(running)[:, :, None] * jnp.einsum(
        "hta,hab->htb", queries_h.astype(jnp.float32), incoming, precision=highest
    )
    attention = jnp.einsum("hts,hsb->htb", scores, values_f, precision=highest) + carried
    normed_h = head_norm(attention, head_gain.reshape(heads, 1, head_dim))
    normed = jnp.transpose(normed_h, (1, 0, 2)).reshape(seq_len, heads * head_dim)

    per_dev = dev_count * half
    flat = ids_all.reshape(dev_count, tok_count * top_count)
    rank = slot_ranks(flat, experts)
    source = jnp.arange(dev_count, dtype=jnp.int32)[:, None]
    slot_index = (flat * PAIR + rank // half) * per_dev + source * half + rank % half
    token_local = source * tok_count + jnp.arange(tok_count * top_count, dtype=jnp.int32)[None, :] // top_count
    slot_token = (
        jnp.full((dev_count * per_dev,), seq_len, jnp.int32)
        .at[slot_index.reshape(-1)]
        .set(token_local.reshape(-1))
    )
    padded = jnp.concatenate([normed, jnp.zeros((1, normed.shape[1]), normed.dtype)], axis=0)
    send_rows = padded[slot_token].reshape(dev_count, per_dev, -1)
    arrived = lax.all_to_all(send_rows, DEV_AXES, split_axis=0, concat_axis=0, tiled=True)
    gate_up_far, arrived = lax.optimization_barrier((gate_up_far, arrived))
    gate_up_far = lax.all_gather(gate_up_far, "c", axis=2, tiled=True)
    down_core, arrived = lax.optimization_barrier((down_core, arrived))
    down_far = lax.ppermute(down_core, "p", partner)
    local_rows = jnp.transpose(arrived, (1, 0, 2)).reshape(per_dev, -1)
    width = local_rows.shape[1]
    groups = 1
    for name in TOK_AXES:
        groups *= lax.axis_size(name)
    piece = lax.all_to_all(
        jnp.broadcast_to(local_rows[None], (groups,) + local_rows.shape),
        TOK_AXES,
        split_axis=0,
        concat_axis=0,
        tiled=True,
    ).reshape(groups * per_dev, width)
    down_far, piece = lax.optimization_barrier((down_far, piece))

    def hidden_of(weights):
        gate_part = jnp.dot(piece, weights[0], preferred_element_type=jnp.float32)
        up_part = jnp.dot(piece, weights[1], preferred_element_type=jnp.float32)
        return (jax.nn.silu(gate_part) * up_part).astype(jnp.bfloat16)

    hidden_all = jnp.concatenate([hidden_of(gate_up_core), hidden_of(gate_up_far)], axis=1)
    down_all = jnp.concatenate([down_core, down_far], axis=0)
    term = jnp.dot(hidden_all, down_all, preferred_element_type=jnp.float32).astype(jnp.bfloat16)
    parts = lax.all_to_all(
        term.reshape(groups, per_dev, width), TOK_AXES, split_axis=0, concat_axis=0, tiled=True
    )
    summed = jnp.sum(parts.astype(jnp.float32), axis=0).astype(jnp.bfloat16)
    returned = lax.all_to_all(
        summed.reshape(dev_count, half, width),
        DEV_AXES,
        split_axis=0,
        concat_axis=0,
        tiled=True,
    )
    own = lax.axis_index(DEV_AXES)
    own_flat = lax.dynamic_index_in_dim(flat, own, 0, False)
    own_rank = lax.dynamic_index_in_dim(rank, own, 0, False)
    pick_index = own_flat * capacity + own_rank
    picked = returned.reshape(dev_count * half, width)[pick_index].reshape(
        tok_count, top_count, width
    )
    combined = jnp.sum(picked.astype(jnp.float32) * expert_weights[:, :, None], axis=1)
    return combined.astype(jnp.bfloat16)


def split_mesh(mesh):
    devices = mesh.devices
    seq_count, dev_count = devices.shape
    cores = 2
    xs = 4
    flat = devices.reshape(-1)
    if hasattr(flat[0], "coords"):
        cores = len({int(getattr(d, "core_on_chip", 0)) for d in flat})
        xs = len({int(d.coords[0]) for d in flat})
    ys = seq_count // (xs * cores)
    shape = (ys, xs, cores, dev_count // PAIR, PAIR)
    return Mesh(devices.reshape(shape), ("y", "x", "c", "e", "p"))


def solution(mesh):
    fine = split_mesh(mesh)
    seq = SEQ_AXES
    in_specs = (
        P(seq, DEV_AXES),
        P(seq, DEV_AXES),
        P(seq, DEV_AXES),
        P(seq, DEV_AXES),
        P(DEV_AXES),
        P(DEV_AXES, None, seq),
        P(DEV_AXES, None, seq),
        P(DEV_AXES, seq, None),
        P(seq + DEV_AXES, None),
        P(seq + DEV_AXES, None),
    )
    out_specs = P(seq + DEV_AXES, None)
    return jax.shard_map(
        per_device, mesh=fine, in_specs=in_specs, out_specs=out_specs, check_vma=False
    )
```

```python
import jax
import jax.numpy as jnp
import numpy as np
from jax import lax
from jax.sharding import Mesh
from jax.sharding import PartitionSpec as P

PAIR = 2

highest = lax.Precision.HIGH

SEQ_AXES = ("y", "x", "c")
TOK_AXES = ("y", "x")
DEV_AXES = ("e", "p")


def chain_join(earlier, later):
    scale = jnp.exp(later[:, -1:, :])
    state = scale * earlier[:, :-1, :] + later[:, :-1, :]
    return jnp.concatenate([state, earlier[:, -1:, :] + later[:, -1:, :]], axis=1)


def shifted(value, shift, count):
    pairs = [(i, i + shift) for i in range(count - shift)]
    return lax.ppermute(value.astype(jnp.bfloat16), SEQ_AXES, pairs).astype(value.dtype)


def carried_in(log_total, local_state, count):
    width = local_state.shape[-1]
    window = jnp.concatenate(
        [local_state, jnp.broadcast_to(log_total[:, None, None], (log_total.shape[0], 1, width))],
        axis=1,
    )
    earlier = None
    shift = 1
    while shift < count:
        arrived = shifted(window, shift, count)
        earlier = arrived if earlier is None else chain_join(arrived, earlier)
        if 2 * shift < count:
            window = chain_join(arrived, window)
        shift *= 2
    return earlier[:, :-1, :]


def head_norm(attention, gain):
    square_mean = jnp.mean(attention * attention, axis=-1, keepdims=True)
    return (attention * lax.rsqrt(square_mean + 1e-06) * gain).astype(jnp.bfloat16)


def slot_ranks(flat_experts, experts):
    onehot = (flat_experts[..., None] == jnp.arange(experts, dtype=jnp.int32)).astype(jnp.int32)
    before = jnp.cumsum(onehot, axis=-2) - onehot
    return jnp.sum(before * onehot, axis=-1)


def per_device(
    queries,
    key_vectors,
    value_vectors,
    log_decay,
    head_gain,
    gate_weight,
    up_weight,
    down_weight,
    expert_ids,
    expert_weights,
):
    count = 1
    for name in SEQ_AXES:
        count *= lax.axis_size(name)
    dev_count = lax.axis_size("e") * lax.axis_size("p")
    experts = dev_count // PAIR

    ids_all = lax.all_gather(expert_ids, DEV_AXES, axis=0, tiled=False)
    partner = [(0, 1), (1, 0)]
    gate_up = jnp.stack([gate_weight[0], up_weight[0]])
    gate_up, ids_all = lax.optimization_barrier((gate_up, ids_all))
    gate_up_core = lax.all_gather(gate_up, "c", axis=2, tiled=True)
    down_core = lax.all_gather(down_weight[0], "c", axis=0, tiled=True)
    gate_up_far = lax.ppermute(gate_up, "p", partner)

    tok_count = expert_ids.shape[0]
    top_count = expert_ids.shape[1]
    capacity = max(2, (3 * tok_count * top_count + 2 * experts - 1) // (2 * experts))
    capacity = -(-capacity // PAIR) * PAIR
    half = capacity // PAIR

    seq_len = queries.shape[0]
    heads = log_decay.shape[1]
    head_dim = queries.shape[1] // heads
    queries_h = jnp.transpose(queries.reshape(seq_len, heads, head_dim), (1, 0, 2))
    keys_h = jnp.transpose(key_vectors.reshape(seq_len, heads, head_dim), (1, 0, 2))
    values_h = jnp.transpose(value_vectors.reshape(seq_len, heads, head_dim), (1, 0, 2))
    decay_h = jnp.transpose(log_decay, (1, 0))
    running = jnp.cumsum(decay_h, axis=1)
    log_total = running[:, -1]
    tail_decay = jnp.exp(log_total[:, None] - running)
    keys_f = keys_h.astype(jnp.float32)
    values_f = values_h.astype(jnp.float32)
    local_state = jnp.einsum(
        "hsa,hsb->hab", keys_f * tail_decay[:, :, None], values_f, precision=highest
    )
    incoming = carried_in(log_total, local_state, count)

    causal = jnp.arange(seq_len)[:, None] >= jnp.arange(seq_len)[None, :]
    spread = jnp.where(causal[None], running[:, :, None] - running[:, None, :], 0.0)
    factors = jnp.where(causal[None], jnp.exp(spread), 0.0)
    scores = (
        jnp.einsum("hta,hsa->hts", queries_h, keys_h, preferred_element_type=jnp.float32) * factors
    )
    carried = jnp.exp(running)[:, :, None] * jnp.einsum(
        "hta,hab->htb", queries_h.astype(jnp.float32), incoming, precision=highest
    )
    attention = jnp.einsum("hts,hsb->htb", scores, values_f, precision=highest) + carried
    normed_h = head_norm(attention, head_gain.reshape(heads, 1, head_dim))
    normed = jnp.transpose(normed_h, (1, 0, 2)).reshape(seq_len, heads * head_dim)

    per_dev = dev_count * half
    flat = ids_all.reshape(dev_count, tok_count * top_count)
    rank = slot_ranks(flat, experts)
    source = jnp.arange(dev_count, dtype=jnp.int32)[:, None]
    slot_index = (flat * PAIR + rank // half) * per_dev + source * half + rank % half
    token_local = source * tok_count + jnp.arange(tok_count * top_count, dtype=jnp.int32)[None, :] // top_count
    slot_token = (
        jnp.full((dev_count * per_dev,), seq_len, jnp.int32)
        .at[slot_index.reshape(-1)]
        .set(token_local.reshape(-1))
    )
    padded = jnp.concatenate([normed, jnp.zeros((1, normed.shape[1]), normed.dtype)], axis=0)
    send_rows = padded[slot_token].reshape(dev_count, per_dev, -1)
    arrived = lax.all_to_all(send_rows, DEV_AXES, split_axis=0, concat_axis=0, tiled=True)
    gate_up_far, arrived = lax.optimization_barrier((gate_up_far, arrived))
    gate_up_far = lax.all_gather(gate_up_far, "c", axis=2, tiled=True)
    down_core, arrived = lax.optimization_barrier((down_core, arrived))
    down_far = lax.ppermute(down_core, "p", partner)
    local_rows = jnp.transpose(arrived, (1, 0, 2)).reshape(per_dev, -1)
    width = local_rows.shape[1]
    groups = 1
    for name in TOK_AXES:
        groups *= lax.axis_size(name)
    piece = lax.all_to_all(
        jnp.broadcast_to(local_rows[None], (groups,) + local_rows.shape),
        TOK_AXES,
        split_axis=0,
        concat_axis=0,
        tiled=True,
    ).reshape(groups * per_dev, width)
    down_far, piece = lax.optimization_barrier((down_far, piece))

    def hidden_of(weights):
        gate_part = jnp.dot(piece, weights[0], preferred_element_type=jnp.float32)
        up_part = jnp.dot(piece, weights[1], preferred_element_type=jnp.float32)
        return (jax.nn.silu(gate_part) * up_part).astype(jnp.bfloat16)

    hidden_all = jnp.concatenate([hidden_of(gate_up_core), hidden_of(gate_up_far)], axis=1)
    down_all = jnp.concatenate([down_core, down_far], axis=0)
    term = jnp.dot(hidden_all, down_all, preferred_element_type=jnp.float32).astype(jnp.bfloat16)
    parts = lax.all_to_all(
        term.reshape(groups, per_dev, width), TOK_AXES, split_axis=0, concat_axis=0, tiled=True
    )
    summed = jnp.sum(parts.astype(jnp.float32), axis=0).astype(jnp.bfloat16)
    returned = lax.all_to_all(
        summed.reshape(dev_count, half, width),
        DEV_AXES,
        split_axis=0,
        concat_axis=0,
        tiled=True,
    )
    own = lax.axis_index(DEV_AXES)
    own_flat = lax.dynamic_index_in_dim(flat, own, 0, False)
    own_rank = lax.dynamic_index_in_dim(rank, own, 0, False)
    pick_index = own_flat * capacity + own_rank
    picked = returned.reshape(dev_count * half, width)[pick_index].reshape(
        tok_count, top_count, width
    )
    combined = jnp.sum(picked.astype(jnp.float32) * expert_weights[:, :, None], axis=1)
    return combined.astype(jnp.bfloat16)


def split_mesh(mesh):
    devices = mesh.devices
    seq_count, dev_count = devices.shape
    cores = 2
    xs = 4
    flat = devices.reshape(-1)
    if hasattr(flat[0], "coords"):
        cores = len({int(getattr(d, "core_on_chip", 0)) for d in flat})
        xs = len({int(d.coords[0]) for d in flat})
    ys = seq_count // (xs * cores)
    shape = (ys, xs, cores, dev_count // PAIR, PAIR)
    return Mesh(devices.reshape(shape), ("y", "x", "c", "e", "p"))


def solution(mesh):
    fine = split_mesh(mesh)
    seq = SEQ_AXES
    in_specs = (
        P(seq, DEV_AXES),
        P(seq, DEV_AXES),
        P(seq, DEV_AXES),
        P(seq, DEV_AXES),
        P(DEV_AXES),
        P(DEV_AXES, None, seq),
        P(DEV_AXES, None, seq),
        P(DEV_AXES, seq, None),
        P(seq + DEV_AXES, None),
        P(seq + DEV_AXES, None),
    )
    out_specs = P(seq + DEV_AXES, None)
    return jax.shard_map(
        per_device, mesh=fine, in_specs=in_specs, out_specs=out_specs, check_vma=False
    )
```

```python
import jax
import jax.numpy as jnp
import numpy as np
from jax import lax
from jax.sharding import Mesh
from jax.sharding import PartitionSpec as P

PAIR = 2

highest = lax.Precision.HIGH

SEQ_AXES = ("y", "x", "c")
TOK_AXES = ("y", "x")
DEV_AXES = ("e", "p")


def chain_join(earlier, later):
    scale = jnp.exp(later[:, -1:, :])
    state = scale * earlier[:, :-1, :] + later[:, :-1, :]
    return jnp.concatenate([state, earlier[:, -1:, :] + later[:, -1:, :]], axis=1)


def shifted(value, shift, count):
    pairs = [(i, i + shift) for i in range(count - shift)]
    return lax.ppermute(value.astype(jnp.bfloat16), SEQ_AXES, pairs).astype(value.dtype)


def carried_in(log_total, local_state, count):
    width = local_state.shape[-1]
    window = jnp.concatenate(
        [local_state, jnp.broadcast_to(log_total[:, None, None], (log_total.shape[0], 1, width))],
        axis=1,
    )
    earlier = None
    shift = 1
    while shift < count:
        arrived = shifted(window, shift, count)
        earlier = arrived if earlier is None else chain_join(arrived, earlier)
        if 2 * shift < count:
            window = chain_join(arrived, window)
        shift *= 2
    return earlier[:, :-1, :]


def head_norm(attention, gain):
    square_mean = jnp.mean(attention * attention, axis=-1, keepdims=True)
    return (attention * lax.rsqrt(square_mean + 1e-06) * gain).astype(jnp.bfloat16)


def slot_ranks(flat_experts, experts):
    onehot = (flat_experts[..., None] == jnp.arange(experts, dtype=jnp.int32)).astype(jnp.int32)
    before = jnp.cumsum(onehot, axis=-2) - onehot
    return jnp.sum(before * onehot, axis=-1)


def per_device(
    queries,
    key_vectors,
    value_vectors,
    log_decay,
    head_gain,
    gate_weight,
    up_weight,
    down_weight,
    expert_ids,
    expert_weights,
):
    count = 1
    for name in SEQ_AXES:
        count *= lax.axis_size(name)
    dev_count = lax.axis_size("e") * lax.axis_size("p")
    experts = dev_count // PAIR

    ids_all = lax.all_gather(expert_ids, DEV_AXES, axis=0, tiled=False)
    partner = [(0, 1), (1, 0)]
    gate_up = jnp.stack([gate_weight[0], up_weight[0]])
    gate_up, ids_all = lax.optimization_barrier((gate_up, ids_all))
    gate_up_core = lax.all_gather(gate_up, "c", axis=2, tiled=True)
    down_core = lax.all_gather(down_weight[0], "c", axis=0, tiled=True)
    gate_up_far = lax.ppermute(gate_up, "p", partner)

    tok_count = expert_ids.shape[0]
    top_count = expert_ids.shape[1]
    capacity = max(2, (3 * tok_count * top_count + 2 * experts - 1) // (2 * experts))
    capacity = -(-capacity // PAIR) * PAIR
    half = capacity // PAIR

    seq_len = queries.shape[0]
    heads = log_decay.shape[1]
    head_dim = queries.shape[1] // heads
    queries_h = jnp.transpose(queries.reshape(seq_len, heads, head_dim), (1, 0, 2))
    keys_h = jnp.transpose(key_vectors.reshape(seq_len, heads, head_dim), (1, 0, 2))
    values_h = jnp.transpose(value_vectors.reshape(seq_len, heads, head_dim), (1, 0, 2))
    decay_h = jnp.transpose(log_decay, (1, 0))
    running = jnp.cumsum(decay_h, axis=1)
    log_total = running[:, -1]
    tail_decay = jnp.exp(log_total[:, None] - running)
    keys_f = keys_h.astype(jnp.float32)
    values_f = values_h.astype(jnp.float32)
    local_state = jnp.einsum(
        "hsa,hsb->hab", keys_f * tail_decay[:, :, None], values_f, precision=highest
    )
    incoming = carried_in(log_total, local_state, count)

    causal = jnp.arange(seq_len)[:, None] >= jnp.arange(seq_len)[None, :]
    spread = jnp.where(causal[None], running[:, :, None] - running[:, None, :], 0.0)
    factors = jnp.where(causal[None], jnp.exp(spread), 0.0)
    scores = (
        jnp.einsum("hta,hsa->hts", queries_h, keys_h, preferred_element_type=jnp.float32) * factors
    )
    carried = jnp.exp(running)[:, :, None] * jnp.einsum(
        "hta,hab->htb", queries_h.astype(jnp.float32), incoming, precision=highest
    )
    attention = jnp.einsum("hts,hsb->htb", scores, values_f, precision=highest) + carried
    normed_h = head_norm(attention, head_gain.reshape(heads, 1, head_dim))
    normed = jnp.transpose(normed_h, (1, 0, 2)).reshape(seq_len, heads * head_dim)

    per_dev = dev_count * half
    flat = ids_all.reshape(dev_count, tok_count * top_count)
    rank = slot_ranks(flat, experts)
    source = jnp.arange(dev_count, dtype=jnp.int32)[:, None]
    slot_index = (flat * PAIR + rank // half) * per_dev + source * half + rank % half
    token_local = source * tok_count + jnp.arange(tok_count * top_count, dtype=jnp.int32)[None, :] // top_count
    slot_token = (
        jnp.full((dev_count * per_dev,), seq_len, jnp.int32)
        .at[slot_index.reshape(-1)]
        .set(token_local.reshape(-1))
    )
    send_rows = jnp.take(normed, slot_token, axis=0, mode="fill", fill_value=0).reshape(
        dev_count, per_dev, -1
    )
    arrived = lax.all_to_all(send_rows, DEV_AXES, split_axis=0, concat_axis=0, tiled=True)
    gate_up_far, arrived = lax.optimization_barrier((gate_up_far, arrived))
    gate_up_far = lax.all_gather(gate_up_far, "c", axis=2, tiled=True)
    down_core, arrived = lax.optimization_barrier((down_core, arrived))
    down_far = lax.ppermute(down_core, "p", partner)
    local_rows = jnp.transpose(arrived, (1, 0, 2)).reshape(per_dev, -1)
    width = local_rows.shape[1]
    groups = 1
    for name in TOK_AXES:
        groups *= lax.axis_size(name)
    piece = lax.all_to_all(
        jnp.broadcast_to(local_rows[None], (groups,) + local_rows.shape),
        TOK_AXES,
        split_axis=0,
        concat_axis=0,
        tiled=True,
    ).reshape(groups * per_dev, width)
    down_far, piece = lax.optimization_barrier((down_far, piece))

    def hidden_of(weights):
        gate_part = jnp.dot(piece, weights[0], preferred_element_type=jnp.float32)
        up_part = jnp.dot(piece, weights[1], preferred_element_type=jnp.float32)
        return (jax.nn.silu(gate_part) * up_part).astype(jnp.bfloat16)

    hidden_all = jnp.concatenate([hidden_of(gate_up_core), hidden_of(gate_up_far)], axis=1)
    down_all = jnp.concatenate([down_core, down_far], axis=0)
    term = jnp.dot(hidden_all, down_all, preferred_element_type=jnp.float32).astype(jnp.bfloat16)
    parts = lax.all_to_all(
        term.reshape(groups, per_dev, width), TOK_AXES, split_axis=0, concat_axis=0, tiled=True
    )
    summed = jnp.sum(parts.astype(jnp.float32), axis=0).astype(jnp.bfloat16)
    returned = lax.all_to_all(
        summed.reshape(dev_count, half, width),
        DEV_AXES,
        split_axis=0,
        concat_axis=0,
        tiled=True,
    )
    own = lax.axis_index(DEV_AXES)
    own_flat = lax.dynamic_index_in_dim(flat, own, 0, False)
    own_rank = lax.dynamic_index_in_dim(rank, own, 0, False)
    pick_index = own_flat * capacity + own_rank
    picked = returned.reshape(dev_count * half, width)[pick_index].reshape(
        tok_count, top_count, width
    )
    combined = jnp.sum(picked.astype(jnp.float32) * expert_weights[:, :, None], axis=1)
    return combined.astype(jnp.bfloat16)


def split_mesh(mesh):
    devices = mesh.devices
    seq_count, dev_count = devices.shape
    cores = 2
    xs = 4
    flat = devices.reshape(-1)
    if hasattr(flat[0], "coords"):
        cores = len({int(getattr(d, "core_on_chip", 0)) for d in flat})
        xs = len({int(d.coords[0]) for d in flat})
    ys = seq_count // (xs * cores)
    shape = (ys, xs, cores, dev_count // PAIR, PAIR)
    return Mesh(devices.reshape(shape), ("y", "x", "c", "e", "p"))


def solution(mesh):
    fine = split_mesh(mesh)
    seq = SEQ_AXES
    in_specs = (
        P(seq, DEV_AXES),
        P(seq, DEV_AXES),
        P(seq, DEV_AXES),
        P(seq, DEV_AXES),
        P(DEV_AXES),
        P(DEV_AXES, None, seq),
        P(DEV_AXES, None, seq),
        P(DEV_AXES, seq, None),
        P(seq + DEV_AXES, None),
        P(seq + DEV_AXES, None),
    )
    out_specs = P(seq + DEV_AXES, None)
    return jax.shard_map(
        per_device, mesh=fine, in_specs=in_specs, out_specs=out_specs, check_vma=False
    )
```

```python
import jax
import jax.numpy as jnp
import numpy as np
from jax import lax
from jax.sharding import Mesh
from jax.sharding import PartitionSpec as P

PAIR = 2

highest = lax.Precision.HIGH

SEQ_AXES = ("y", "x", "c")
TOK_AXES = ("y", "x")
DEV_AXES = ("e", "p")


def chain_join(earlier, later):
    rows = jnp.arange(earlier.shape[1])[None, :, None]
    scale = jnp.where(rows < earlier.shape[1] - 1, jnp.exp(later[:, -1:, :]), 1.0)
    return scale * earlier + later


def shifted(value, shift, count):
    pairs = [(i, i + shift) for i in range(count - shift)]
    return lax.ppermute(value.astype(jnp.bfloat16), SEQ_AXES, pairs).astype(value.dtype)


def carried_in(log_total, local_state, count):
    width = local_state.shape[-1]
    window = jnp.concatenate(
        [local_state, jnp.broadcast_to(log_total[:, None, None], (log_total.shape[0], 1, width))],
        axis=1,
    )
    earlier = None
    shift = 1
    while shift < count:
        arrived = shifted(window, shift, count)
        earlier = arrived if earlier is None else chain_join(arrived, earlier)
        if 2 * shift < count:
            window = chain_join(arrived, window)
        shift *= 2
    return earlier[:, :-1, :]


def head_norm(attention, gain):
    square_mean = jnp.mean(attention * attention, axis=-1, keepdims=True)
    return (attention * lax.rsqrt(square_mean + 1e-06) * gain).astype(jnp.bfloat16)


def slot_ranks(flat_experts, experts):
    onehot = (flat_experts[..., None] == jnp.arange(experts, dtype=jnp.int32)).astype(jnp.int32)
    before = jnp.cumsum(onehot, axis=-2) - onehot
    return jnp.sum(before * onehot, axis=-1)


def per_device(
    queries,
    key_vectors,
    value_vectors,
    log_decay,
    head_gain,
    gate_weight,
    up_weight,
    down_weight,
    expert_ids,
    expert_weights,
):
    count = 1
    for name in SEQ_AXES:
        count *= lax.axis_size(name)
    dev_count = lax.axis_size("e") * lax.axis_size("p")
    experts = dev_count // PAIR

    ids_all = lax.all_gather(expert_ids, DEV_AXES, axis=0, tiled=False)
    partner = [(0, 1), (1, 0)]
    gate_up = jnp.stack([gate_weight[0], up_weight[0]])
    gate_up, ids_all = lax.optimization_barrier((gate_up, ids_all))
    gate_up_core = lax.all_gather(gate_up, "c", axis=2, tiled=True)
    down_core = lax.all_gather(down_weight[0], "c", axis=0, tiled=True)
    gate_up_far = lax.ppermute(gate_up, "p", partner)

    tok_count = expert_ids.shape[0]
    top_count = expert_ids.shape[1]
    capacity = max(2, (3 * tok_count * top_count + 2 * experts - 1) // (2 * experts))
    capacity = -(-capacity // PAIR) * PAIR
    half = capacity // PAIR

    seq_len = queries.shape[0]
    heads = log_decay.shape[1]
    head_dim = queries.shape[1] // heads
    queries_h = jnp.transpose(queries.reshape(seq_len, heads, head_dim), (1, 0, 2))
    keys_h = jnp.transpose(key_vectors.reshape(seq_len, heads, head_dim), (1, 0, 2))
    values_h = jnp.transpose(value_vectors.reshape(seq_len, heads, head_dim), (1, 0, 2))
    decay_h = jnp.transpose(log_decay, (1, 0))
    running = jnp.cumsum(decay_h, axis=1)
    log_total = running[:, -1]
    tail_decay = jnp.exp(log_total[:, None] - running)
    keys_f = keys_h.astype(jnp.float32)
    values_f = values_h.astype(jnp.float32)
    local_state = jnp.einsum(
        "hsa,hsb->hab", keys_f * tail_decay[:, :, None], values_f, precision=highest
    )
    incoming = carried_in(log_total, local_state, count)

    causal = jnp.arange(seq_len)[:, None] >= jnp.arange(seq_len)[None, :]
    spread = jnp.where(causal[None], running[:, :, None] - running[:, None, :], 0.0)
    factors = jnp.where(causal[None], jnp.exp(spread), 0.0)
    scores = (
        jnp.einsum("hta,hsa->hts", queries_h, keys_h, preferred_element_type=jnp.float32) * factors
    )
    carried = jnp.exp(running)[:, :, None] * jnp.einsum(
        "hta,hab->htb", queries_h.astype(jnp.float32), incoming, precision=highest
    )
    attention = jnp.einsum("hts,hsb->htb", scores, values_f, precision=highest) + carried
    normed_h = head_norm(attention, head_gain.reshape(heads, 1, head_dim))
    normed = jnp.transpose(normed_h, (1, 0, 2)).reshape(seq_len, heads * head_dim)

    per_dev = dev_count * half
    flat = ids_all.reshape(dev_count, tok_count * top_count)
    rank = slot_ranks(flat, experts)
    source = jnp.arange(dev_count, dtype=jnp.int32)[:, None]
    slot_index = (flat * PAIR + rank // half) * per_dev + source * half + rank % half
    token_local = source * tok_count + jnp.arange(tok_count * top_count, dtype=jnp.int32)[None, :] // top_count
    slot_token = (
        jnp.full((dev_count * per_dev,), seq_len, jnp.int32)
        .at[slot_index.reshape(-1)]
        .set(token_local.reshape(-1))
    )
    padded = jnp.concatenate([normed, jnp.zeros((1, normed.shape[1]), normed.dtype)], axis=0)
    send_rows = padded[slot_token].reshape(dev_count, per_dev, -1)
    arrived = lax.all_to_all(send_rows, DEV_AXES, split_axis=0, concat_axis=0, tiled=True)
    gate_up_far, arrived = lax.optimization_barrier((gate_up_far, arrived))
    gate_up_far = lax.all_gather(gate_up_far, "c", axis=2, tiled=True)
    down_core, arrived = lax.optimization_barrier((down_core, arrived))
    down_far = lax.ppermute(down_core, "p", partner)
    local_rows = jnp.transpose(arrived, (1, 0, 2)).reshape(per_dev, -1)
    width = local_rows.shape[1]
    groups = 1
    for name in TOK_AXES:
        groups *= lax.axis_size(name)
    piece = lax.all_to_all(
        jnp.broadcast_to(local_rows[None], (groups,) + local_rows.shape),
        TOK_AXES,
        split_axis=0,
        concat_axis=0,
        tiled=True,
    ).reshape(groups * per_dev, width)
    down_far, piece = lax.optimization_barrier((down_far, piece))

    def hidden_of(weights):
        gate_part = jnp.dot(piece, weights[0], preferred_element_type=jnp.float32)
        up_part = jnp.dot(piece, weights[1], preferred_element_type=jnp.float32)
        return (jax.nn.silu(gate_part) * up_part).astype(jnp.bfloat16)

    hidden_all = jnp.concatenate([hidden_of(gate_up_core), hidden_of(gate_up_far)], axis=1)
    down_all = jnp.concatenate([down_core, down_far], axis=0)
    term = jnp.dot(hidden_all, down_all, preferred_element_type=jnp.float32).astype(jnp.bfloat16)
    parts = lax.all_to_all(
        term.reshape(groups, per_dev, width), TOK_AXES, split_axis=0, concat_axis=0, tiled=True
    )
    summed = jnp.sum(parts.astype(jnp.float32), axis=0).astype(jnp.bfloat16)
    returned = lax.all_to_all(
        summed.reshape(dev_count, half, width),
        DEV_AXES,
        split_axis=0,
        concat_axis=0,
        tiled=True,
    )
    own = lax.axis_index(DEV_AXES)
    own_flat = lax.dynamic_index_in_dim(flat, own, 0, False)
    own_rank = lax.dynamic_index_in_dim(rank, own, 0, False)
    pick_index = own_flat * capacity + own_rank
    picked = returned.reshape(dev_count * half, width)[pick_index].reshape(
        tok_count, top_count, width
    )
    combined = jnp.sum(picked.astype(jnp.float32) * expert_weights[:, :, None], axis=1)
    return combined.astype(jnp.bfloat16)


def split_mesh(mesh):
    devices = mesh.devices
    seq_count, dev_count = devices.shape
    cores = 2
    xs = 4
    flat = devices.reshape(-1)
    if hasattr(flat[0], "coords"):
        cores = len({int(getattr(d, "core_on_chip", 0)) for d in flat})
        xs = len({int(d.coords[0]) for d in flat})
    ys = seq_count // (xs * cores)
    shape = (ys, xs, cores, dev_count // PAIR, PAIR)
    return Mesh(devices.reshape(shape), ("y", "x", "c", "e", "p"))


def solution(mesh):
    fine = split_mesh(mesh)
    seq = SEQ_AXES
    in_specs = (
        P(seq, DEV_AXES),
        P(seq, DEV_AXES),
        P(seq, DEV_AXES),
        P(seq, DEV_AXES),
        P(DEV_AXES),
        P(DEV_AXES, None, seq),
        P(DEV_AXES, None, seq),
        P(DEV_AXES, seq, None),
        P(seq + DEV_AXES, None),
        P(seq + DEV_AXES, None),
    )
    out_specs = P(seq + DEV_AXES, None)
    return jax.shard_map(
        per_device, mesh=fine, in_specs=in_specs, out_specs=out_specs, check_vma=False
    )
```
